256 devices in a mesh: region: 8 (over z), row: 32 (over y, x, core).
Axes of the slice: x: 4, y: 4, z: 8, core: 2. Of those that a mesh axis runs over, the one named last changes fastest.
Arguments:
- state0: float32 [32, 131072], P(None, ('region', 'row')), may hold values from -6 to 6
- drive: bfloat16 [32, 131072], P(None, ('region', 'row')), may hold values from -6 to 6
- cotangent: float32 [32, 131072], P(None, ('region', 'row')), may hold values from -6 to 6
- excitatory: int32 [131072], P(('region', 'row')), may hold values 0 or 1
- tile_vals: bfloat16 [1024, 24, 128, 128], P(('region', 'row')), may hold values from 0.0039978027 to 0.039794922
- tile_cols: int32 [1024, 24], P(('region', 'row')), may hold values from 0 to 159
- tile_count: int32 [1024], P(('region', 'row')), may hold values from 1 to 24, as said below
- boundary_rows: int32 [8, 32, 8, 16], P('region', 'row'), may hold values from 0 to 511, as said below
- u_factor: bfloat16 [32, 131072], P(None, ('region', 'row')), may hold values from -1 to 1
- v_factor: bfloat16 [32, 131072], P(None, ('region', 'row')), may hold values from -0.015625 to 0.015625
Outputs:
- final_state: float32 [32, 131072], P(None, ('region', 'row'))
- grad_u: float32 [32, 131072], P(None, ('region', 'row'))
- grad_v: float32 [32, 131072], P(None, ('region', 'row'))
The draws below stay inside these ranges and needn't reach their ends.
Inputs may be any that keep to these rules, and one draw needn't show every extreme that they name: tile_count[q] tiles of row tile q are live; its tiles j >= tile_count[q] take no part; the most, 24, is reached in every draw. `boundary_rows`: the 16 rows of one list are distinct. tile_cols[q, j] numbers a tile of 128 extended columns of the group of row tile q.
All inputs are finite; a program needn't handle non-finite values. No bound on the sum of `excitatory` on one device may be relied on, other than what follows from the above.
Results may differ from the reference program's by a relative error of at most 0.0055.
Values may be sent and summed in bfloat16 or wider, within the bound.
No kernel may reach another device: no remote copies, remote signals or barrier semaphores. Data moves between devices by JAX's collectives and lax.ppermute only.
A program may use at most 64 MiB of HBM per device.

```python
import math
import jax
import jax.numpy as jnp
from jax import lax

BATCH = 32
ROWS_DEV = 512
KMAX = 24
BOUND = 128
RANK = 32
STEPS = 4
NEURONS = 131072
ROWTILES = 1024
REGION_TILES = 128
COLT = 160
BSRC = 16
GROUPS = 8
ROW_DEVS = 32
N_REGION = 8
N_ROW = 32


def draw_tile_count(key, part):
    key_level, key_jitter, key_peak = jax.random.split(key, 3)
    levels = jax.random.randint(key_level, (ROWTILES // REGION_TILES,), KMAX // 4, KMAX + 1)
    jitter_width = KMAX // 8
    jitter = jax.random.randint(key_jitter, (ROWTILES,), -jitter_width, jitter_width + 1)
    counts = jnp.clip(jnp.repeat(levels, REGION_TILES) + jitter, 1, KMAX)
    peak_row = jax.random.randint(key_peak, (), 0, ROWTILES)
    return counts.at[peak_row].set(KMAX).astype(jnp.int32)


def draw_boundary_rows(key, part):
    list_count = GROUPS * ROW_DEVS * GROUPS
    keys_all = jax.random.split(key, list_count)
    chosen = jax.vmap(lambda one_key: jax.random.permutation(one_key, ROWS_DEV)[:BSRC])(keys_all)
    return chosen.reshape(GROUPS, ROW_DEVS, GROUPS, BSRC).astype(jnp.int32)


def touch_ends(values, own_key, smallest, high):
    index_at = [jax.random.randint(jax.random.fold_in(own_key, axis), (), 0, length) for axis, length in enumerate(values.shape)]
    main_axis = values.shape.index(max(values.shape))
    beside = index_at[:main_axis] + [(index_at[main_axis] + 1) % values.shape[main_axis]] + index_at[main_axis + 1:]
    return values.at[tuple(index_at)].set(smallest).at[tuple(beside)].set(high)


def block_levels(key, extent, pieces, least, top_value):
    factor_of, own = 1.0, jax.random.fold_in(key, 6)
    for axis_at, shards_of in pieces:
        heights = jnp.exp(jax.random.uniform(jax.random.fold_in(own, axis_at), (shards_of,), jnp.float32, least / len(pieces), top_value / len(pieces)))
        factor_of = factor_of * jnp.repeat(heights, extent[axis_at] // shards_of).reshape([-1 if axis == axis_at else 1 for axis in range(len(extent))])
    return factor_of


def bell_draw(own_key, shape, scale, reach, shards=(), kind=jnp.bfloat16):
    drawn = scale * jax.random.normal(own_key, shape, jnp.float32)
    if shards:
        drawn = drawn * block_levels(own_key, shape, shards, -0.22, 0.18)
    return jnp.clip(drawn, -reach, reach).astype(kind)


def setup_inputs(seed: int = 0) -> dict:
    key_list = jax.random.split(jax.random.key(seed), 11)
    return {
        "state0": bell_draw(key_list[0], (BATCH, NEURONS), 1.0, 6.0, ((1, 256),), jnp.float32),
        "drive": bell_draw(key_list[1], (BATCH, NEURONS), 1.0, 6.0, ((1, 256),)),
        "cotangent": bell_draw(key_list[2], (BATCH, NEURONS), 1.0, 6.0, ((1, 256),), jnp.float32),
        "excitatory": touch_ends((jax.random.randint(key_list[3], (NEURONS,), 0, 2) < 1).astype(jnp.int32), jax.random.fold_in(key_list[3], 1), 0, 1),
        "tile_vals": jnp.clip(jnp.exp(math.log(0.039794922) - 2.2979944 * jax.random.uniform(key_list[4], (ROWTILES, KMAX, 128, 128), jnp.float32) ** block_levels(key_list[4], (ROWTILES, KMAX, 128, 128), ((0, 256),), -0.2, 0.2)), 0.0039978027, 0.039794922).astype(jnp.bfloat16),
        "tile_cols": touch_ends(jax.random.randint(key_list[5], (ROWTILES, KMAX), 0, COLT), jax.random.fold_in(key_list[5], 1), 0, COLT - 1).astype(jnp.int32),
        "tile_count": draw_tile_count(jax.random.fold_in(key_list[10], 71), 0),
        "boundary_rows": draw_boundary_rows(jax.random.fold_in(key_list[10], 71), 0),
        "u_factor": bell_draw(key_list[8], (RANK, NEURONS), RANK ** -0.5, 1.0, ((1, 256),)),
        "v_factor": bell_draw(key_list[9], (RANK, NEURONS), NEURONS ** -0.5, 0.015625, ((1, 256),)),
    }


leak = 0.5


def reference(state0, drive, cotangent, excitatory, tile_vals, tile_cols, tile_count, boundary_rows, u_factor, v_factor):
    batch_rows = state0.shape[0]
    groups = N_REGION
    lanes = N_ROW
    region_tiles = ROWTILES // groups
    dev_tiles = ROWS_DEV // 128
    per_lane = (ROWS_DEV + BOUND) // 128
    col_tiles = lanes * per_lane
    polarity = (2 * excitatory - 1).astype(jnp.float32)
    source = jnp.arange(groups, dtype=jnp.int32)[:, None, None, None]
    lane_ids = jnp.arange(lanes, dtype=jnp.int32)[None, :, None, None]
    global_rows = (source * lanes + lane_ids) * ROWS_DEV + boundary_rows
    border_cols = jnp.transpose(global_rows, (2, 1, 0, 3)).reshape(groups, lanes, BOUND).astype(jnp.int32)
    live_all = jnp.arange(KMAX, dtype=jnp.int32)[None, :] < tile_count[:, None]
    live_group = live_all.reshape(groups, region_tiles, KMAX)
    tiles_group = tile_vals.reshape(groups, region_tiles, KMAX, 128, 128)
    cols_group = tile_cols.reshape(groups, region_tiles, KMAX)
    device_of = jnp.broadcast_to((jnp.arange(region_tiles, dtype=jnp.int32) // dev_tiles)[:, None], (region_tiles, KMAX))

    def forward_region(packed):
        ext_cols, tiles_one, cols_one, live_one = packed
        blocks = ext_cols[:, cols_one, :].astype(jnp.float32)
        blocks = jnp.where(live_one[None, :, :, None], blocks, 0.0)
        result = jnp.einsum("brjk,rjik->bri", blocks, tiles_one.astype(jnp.float32))
        return result.reshape(batch_rows, region_tiles * 128)

    def adjoint_region(packed):
        scaled_one, tiles_one, cols_one, live_one = packed
        spread = jnp.einsum("bri,rjik->brjk", scaled_one.astype(jnp.float32), tiles_one.astype(jnp.float32))
        spread = jnp.where(live_one[None, :, :, None], spread, 0.0)
        terms = jnp.zeros((lanes, col_tiles, batch_rows, 128), jnp.float32)
        terms = terms.at[device_of, cols_one].add(jnp.transpose(spread, (1, 2, 0, 3)))
        rounded = lax.optimization_barrier(terms.astype(jnp.bfloat16)).astype(jnp.float32)
        summed = jnp.sum(rounded, axis=0)
        summed = jnp.transpose(summed, (1, 0, 2)).reshape(batch_rows, lanes, per_lane * 128)
        return summed[:, :, :ROWS_DEV], summed[:, :, ROWS_DEV:]

    state = state0
    saved = []
    for moment in range(STEPS):
        rates = jnp.tanh(state)
        signed = (polarity * rates).astype(jnp.bfloat16)
        extended = jnp.concatenate([signed.reshape(batch_rows, groups, lanes, ROWS_DEV), signed[:, border_cols]], axis=3)
        ext_by_group = jnp.transpose(extended.reshape(batch_rows, groups, col_tiles, 128), (1, 0, 2, 3))
        synaptic = lax.map(forward_region, (ext_by_group, tiles_group, cols_group, live_group))
        synaptic = jnp.transpose(synaptic, (1, 0, 2)).reshape(batch_rows, NEURONS)
        latent = jnp.dot(signed, v_factor.T, preferred_element_type=jnp.float32).astype(jnp.bfloat16)
        lowrank = jnp.dot(latent, u_factor, preferred_element_type=jnp.float32)
        saved.append((rates, signed, latent))
        state = state + leak * (-state + synaptic + lowrank + drive.astype(jnp.float32))

    grad_u = jnp.zeros((RANK, NEURONS), jnp.float32)
    grad_v = jnp.zeros((RANK, NEURONS), jnp.float32)
    adjoint = cotangent
    for moment in reversed(range(STEPS)):
        rates, signed, latent = saved[moment]
        scaled = (leak * adjoint).astype(jnp.bfloat16)
        coeffs = jnp.dot(scaled, u_factor.T, preferred_element_type=jnp.float32).astype(jnp.bfloat16)
        scaled_group = jnp.transpose(scaled.reshape(batch_rows, groups, region_tiles, 128), (1, 0, 2, 3))
        own_all, border_all = lax.map(adjoint_region, (scaled_group, tiles_group, cols_group, live_group))
        own_flat = jnp.transpose(own_all, (1, 0, 2, 3)).reshape(batch_rows, NEURONS)
        border_flat = jnp.transpose(border_all, (1, 0, 2, 3)).reshape(batch_rows, groups * lanes * BOUND)
        through = own_flat.at[:, border_cols.reshape(-1)].add(border_flat)
        total_signed = through + jnp.dot(coeffs, v_factor, preferred_element_type=jnp.float32)
        grad_u = grad_u + jnp.dot(latent.T, scaled, preferred_element_type=jnp.float32)
        grad_v = grad_v + jnp.dot(coeffs.T, signed, preferred_element_type=jnp.float32)
        adjoint = (1.0 - leak) * adjoint + (1.0 - rates * rates) * polarity * total_signed
    return (state, grad_u, grad_v)
```

```python
import jax
import jax.numpy as jnp
from jax import lax
from jax.sharding import Mesh
from jax.sharding import PartitionSpec as P

STEPS = 4
ROW = ("row_0", "row_1", "row_2")
REGION_ROW = ("region", "row_0", "row_1", "row_2")


leak = 0.5


def apply_tiles(ext_cols, flat_cols, live_tiles, flat_tiles, row_tiles):
    batch_rows, span_cols = ext_cols.shape
    blocks = ext_cols.reshape(batch_rows, span_cols // 128, 128)[:, flat_cols, :]
    blocks = jnp.where(live_tiles[None, :, None], blocks, jnp.zeros((), blocks.dtype))
    product = jnp.einsum("bsk,sik->bsi", blocks, flat_tiles, preferred_element_type=jnp.float32)
    summed = product.reshape(batch_rows, row_tiles, -1, 128).sum(axis=2)
    return summed.reshape(batch_rows, row_tiles * 128)


def from_each_region(x, me):
    everyone = lax.all_gather(x, "region", axis=0, tiled=False)
    mine = lax.dynamic_index_in_dim(everyone, me, axis=2, keepdims=False)
    return jnp.moveaxis(mine, 0, 1).reshape(x.shape[0], -1)


def local(
    state0,
    drive,
    cotangent,
    excitatory,
    tile_vals,
    tile_cols,
    tile_count,
    boundary_rows,
    u_factor,
    v_factor,
):
    lanes = lax.axis_size(ROW)
    groups = lax.axis_size("region")
    me = lax.axis_index("region")
    own_rows = state0.shape[1]
    own_tiles = own_rows // 128
    row_tiles = tile_vals.shape[0]
    chosen = boundary_rows.reshape(-1)
    bound_cols = chosen.shape[0]
    bound_tiles = bound_cols // 128
    per_lane = own_tiles + bound_tiles
    lane_of = tile_cols // per_lane
    at_lane = tile_cols % per_lane
    remapped = jnp.where(
        at_lane < own_tiles, lane_of * own_tiles + at_lane, lanes * own_tiles + lane_of * bound_tiles + at_lane - own_tiles
    )
    flat_cols = remapped.reshape(-1)
    live_grid = jnp.arange(tile_cols.shape[1], dtype=jnp.int32)[None, :] < tile_count[:, None]
    live_tiles = live_grid.reshape(-1)
    flat_tiles = tile_vals.reshape(-1, 128, 128)
    polarity = (2 * excitatory - 1).astype(jnp.float32)
    state = state0
    saved = []
    for moment in range(STEPS):
        rates = jnp.tanh(state)
        signed = (polarity * rates).astype(jnp.bfloat16)
        batch_rows = signed.shape[0]
        gathered_own = lax.all_gather(signed, ROW, axis=1, tiled=True)
        outgoing = jnp.take(signed, chosen, axis=1).reshape(batch_rows, groups, -1)
        incoming = from_each_region(outgoing, me)
        latent = lax.psum(jnp.dot(signed, v_factor.T, preferred_element_type=jnp.float32), REGION_ROW)
        gathered_border = lax.all_gather(incoming, ROW, axis=1, tiled=True)
        gathered = jnp.concatenate([gathered_own, gathered_border], axis=1)
        synaptic = apply_tiles(gathered, flat_cols, live_tiles, flat_tiles, row_tiles)
        latent_b = latent.astype(jnp.bfloat16)
        lowrank = jnp.dot(latent_b, u_factor, preferred_element_type=jnp.float32)
        saved.append((rates, signed, latent_b))
        state = state + leak * (-state + synaptic + lowrank + drive.astype(jnp.float32))
    grad_u = jnp.zeros((u_factor.shape[0], own_rows), jnp.float32)
    grad_v = jnp.zeros((v_factor.shape[0], own_rows), jnp.float32)
    adjoint = cotangent
    for moment in reversed(range(STEPS)):
        rates, signed, latent_b = saved[moment]
        scaled_b = (leak * adjoint).astype(jnp.bfloat16)
        coeffs = lax.psum(jnp.dot(scaled_b, u_factor.T, preferred_element_type=jnp.float32), REGION_ROW)
        coeffs_b = coeffs.astype(jnp.bfloat16)
        batch_rows = scaled_b.shape[0]
        spread = jnp.einsum(
            "bri,rjik->brjk",
            scaled_b.reshape(batch_rows, row_tiles, 128),
            tile_vals,
            preferred_element_type=jnp.float32,
        )
        spread = jnp.where(live_grid[None, :, :, None], spread, 0.0)
        columns = jnp.zeros((batch_rows, lanes * per_lane, 128), jnp.float32)
        columns = columns.at[:, flat_cols, :].add(spread.reshape(batch_rows, -1, 128))
        rounded = columns.astype(jnp.bfloat16).astype(jnp.float32)
        own_cols = rounded[:, : lanes * own_tiles].reshape(batch_rows, -1)
        border_cols = rounded[:, lanes * own_tiles :].reshape(batch_rows, -1)
        border = lax.psum_scatter(border_cols, ROW, scatter_dimension=1, tiled=True)
        returned = from_each_region(border.reshape(batch_rows, groups, -1), me)
        own_part = lax.psum_scatter(own_cols, ROW, scatter_dimension=1, tiled=True)
        through = own_part.at[:, chosen].add(returned)
        total_signed = through + jnp.dot(coeffs_b, v_factor, preferred_element_type=jnp.float32)
        grad_u = grad_u + jnp.dot(latent_b.T, scaled_b, preferred_element_type=jnp.float32)
        grad_v = grad_v + jnp.dot(coeffs_b.T, signed, preferred_element_type=jnp.float32)
        adjoint = (1.0 - leak) * adjoint + (1.0 - rates * rates) * polarity * total_signed
    return (state, grad_u, grad_v)


def solution(mesh):
    finer = Mesh(
        mesh.devices.reshape(mesh.shape["region"], 4, 4, 2), ("region", "row_0", "row_1", "row_2")
    )
    in_specs = (
        P(None, REGION_ROW),
        P(None, REGION_ROW),
        P(None, REGION_ROW),
        P(REGION_ROW),
        P(REGION_ROW, None, None, None),
        P(REGION_ROW, None),
        P(REGION_ROW),
        P("region", ROW, None, None),
        P(None, REGION_ROW),
        P(None, REGION_ROW),
    )
    out_specs = (P(None, REGION_ROW), P(None, REGION_ROW), P(None, REGION_ROW))
    return jax.shard_map(local, mesh=finer, in_specs=in_specs, out_specs=out_specs, check_vma=False)
```

```python
import jax
import jax.numpy as jnp
from jax import lax
from jax.sharding import Mesh
from jax.sharding import PartitionSpec as P

STEPS = 4
ROW = ("row_0", "row_1", "row_2")
REGION_ROW = ("region", "row_0", "row_1", "row_2")


leak = 0.5


def from_each_region(chunks, me):
    groups = chunks.shape[0]
    by_shift = [lax.dynamic_index_in_dim(chunks, me, axis=0, keepdims=False)]
    for shift in range(1, groups):
        send = lax.dynamic_index_in_dim(chunks, (me + shift) % groups, axis=0, keepdims=False)
        pairs = [(i, (i + shift) % groups) for i in range(groups)]
        by_shift.append(lax.ppermute(send, "region", pairs))
    by_shift = jnp.stack(by_shift)
    order = (me - jnp.arange(groups, dtype=jnp.int32)) % groups
    return jnp.take(by_shift, order, axis=0)


def split_pair(x):
    high = x.astype(jnp.bfloat16)
    low = (x - high.astype(jnp.float32)).astype(jnp.bfloat16)
    return jnp.concatenate([high, low], axis=-1)


def joined_pair(x):
    half = x.shape[-1] // 2
    return x[..., :half].astype(jnp.float32) + x[..., half:].astype(jnp.float32)


def local(
    state0,
    drive,
    cotangent,
    excitatory,
    tile_vals,
    tile_cols,
    tile_count,
    boundary_rows,
    u_factor,
    v_factor,
):
    lanes = lax.axis_size(ROW)
    groups = lax.axis_size("region")
    me = lax.axis_index("region")
    batch_rows, own_rows = state0.shape
    rank = v_factor.shape[0]
    own_tiles = own_rows // 128
    row_tiles = tile_vals.shape[0]
    chosen = boundary_rows.reshape(-1)
    bound_cols = chosen.shape[0]
    per_lane = own_tiles + bound_cols // 128
    ext_cols = per_lane * 128
    flat_cols = tile_cols.reshape(-1)
    lane_of = flat_cols // per_lane
    at_lane = flat_cols % per_lane
    live_grid = jnp.arange(tile_cols.shape[1], dtype=jnp.int32)[None, :] < tile_count[:, None]
    live_tiles = live_grid.reshape(-1)
    flat_tiles = tile_vals.reshape(-1, 128, 128)
    polarity = (2 * excitatory - 1).astype(jnp.float32)
    state = state0
    saved = []
    for moment in range(STEPS):
        rates = jnp.tanh(state)
        signed = (polarity * rates).astype(jnp.bfloat16)
        outgoing = jnp.take(signed, chosen, axis=1).reshape(batch_rows, groups, -1)
        part_latent = jnp.dot(signed, v_factor.T, preferred_element_type=jnp.float32)
        chunks = jnp.concatenate(
            [
                jnp.moveaxis(outgoing, 1, 0).astype(jnp.float32),
                jnp.broadcast_to(part_latent, (groups, batch_rows, rank)),
            ],
            axis=2,
        )
        got = from_each_region(chunks, me)
        incoming = jnp.moveaxis(got[:, :, : outgoing.shape[2]], 0, 1).reshape(batch_rows, -1).astype(jnp.bfloat16)
        lane_latent = jnp.sum(got[:, :, outgoing.shape[2] :], axis=0)
        payload = jnp.concatenate([signed, incoming, split_pair(lane_latent)], axis=1)
        copies = jnp.broadcast_to(payload, (lanes, *payload.shape))
        gathered = lax.all_to_all(copies, ROW, 0, 0, tiled=True)
        latent = jnp.sum(joined_pair(gathered[:, :, ext_cols:]), axis=0)
        ext = gathered[:, :, :ext_cols].reshape(lanes, batch_rows, per_lane, 128)
        blocks = ext[lane_of, :, at_lane, :]
        blocks = jnp.where(live_tiles[:, None, None], blocks, jnp.zeros((), blocks.dtype))
        product = jnp.einsum("sbk,sik->bsi", blocks, flat_tiles, preferred_element_type=jnp.float32)
        synaptic = product.reshape(batch_rows, row_tiles, -1, 128).sum(axis=2).reshape(batch_rows, own_rows)
        latent_b = latent.astype(jnp.bfloat16)
        lowrank = jnp.dot(latent_b, u_factor, preferred_element_type=jnp.float32)
        saved.append((rates, signed, latent_b))
        state = state + leak * (-state + synaptic + lowrank + drive.astype(jnp.float32))
    grad_u = jnp.zeros((u_factor.shape[0], own_rows), jnp.float32)
    grad_v = jnp.zeros((v_factor.shape[0], own_rows), jnp.float32)
    adjoint = cotangent
    for moment in reversed(range(STEPS)):
        rates, signed, latent_b = saved[moment]
        scaled_b = (leak * adjoint).astype(jnp.bfloat16)
        part_coeff = jnp.dot(scaled_b, u_factor.T, preferred_element_type=jnp.float32)
        spread = jnp.einsum(
            "bri,rjik->brjk",
            scaled_b.reshape(batch_rows, row_tiles, 128),
            tile_vals,
            preferred_element_type=jnp.float32,
        )
        spread = jnp.where(live_grid[None, :, :, None], spread, 0.0)
        columns = jnp.zeros((batch_rows, lanes * per_lane, 128), jnp.float32)
        columns = columns.at[:, flat_cols, :].add(spread.reshape(batch_rows, -1, 128))
        parts = jnp.moveaxis(columns.astype(jnp.bfloat16).reshape(batch_rows, lanes, ext_cols), 1, 0)
        coeff_pair = jnp.broadcast_to(split_pair(part_coeff), (lanes, batch_rows, 2 * rank))
        got = lax.all_to_all(jnp.concatenate([parts, coeff_pair], axis=2), ROW, 0, 0, tiled=True)
        summed = jnp.sum(got[:, :, :ext_cols].astype(jnp.float32), axis=0)
        group_coeff = jnp.sum(joined_pair(got[:, :, ext_cols:]), axis=0)
        own_part = summed[:, :own_rows]
        border = summed[:, own_rows:].reshape(batch_rows, groups, -1)
        chunks = jnp.concatenate(
            [jnp.moveaxis(border, 1, 0), jnp.broadcast_to(group_coeff, (groups, batch_rows, rank))], axis=2
        )
        back = from_each_region(chunks, me)
        returned = jnp.moveaxis(back[:, :, : border.shape[2]], 0, 1).reshape(batch_rows, -1)
        coeffs_b = jnp.sum(back[:, :, border.shape[2] :], axis=0).astype(jnp.bfloat16)
        through = own_part.at[:, chosen].add(returned)
        total_signed = through + jnp.dot(coeffs_b, v_factor, preferred_element_type=jnp.float32)
        grad_u = grad_u + jnp.dot(latent_b.T, scaled_b, preferred_element_type=jnp.float32)
        grad_v = grad_v + jnp.dot(coeffs_b.T, signed, preferred_element_type=jnp.float32)
        adjoint = (1.0 - leak) * adjoint + (1.0 - rates * rates) * polarity * total_signed
    return (state, grad_u, grad_v)


def solution(mesh):
    finer = Mesh(
        mesh.devices.reshape(mesh.shape["region"], 4, 4, 2), ("region", "row_0", "row_1", "row_2")
    )
    in_specs = (
        P(None, REGION_ROW),
        P(None, REGION_ROW),
        P(None, REGION_ROW),
        P(REGION_ROW),
        P(REGION_ROW, None, None, None),
        P(REGION_ROW, None),
        P(REGION_ROW),
        P("region", ROW, None, None),
        P(None, REGION_ROW),
        P(None, REGION_ROW),
    )
    out_specs = (P(None, REGION_ROW), P(None, REGION_ROW), P(None, REGION_ROW))
    return jax.shard_map(local, mesh=finer, in_specs=in_specs, out_specs=out_specs, check_vma=False)
```

```python
import jax
import jax.numpy as jnp
from jax import lax
from jax.sharding import Mesh
from jax.sharding import PartitionSpec as P

STEPS = 4
ROW = ("row_0", "row_1", "row_2")
REGION_ROW = ("region", "row_0", "row_1", "row_2")


leak = 0.5


def from_each_region(chunks):
    return lax.all_to_all(chunks, "region", 0, 0, tiled=True)


def split_pair(x):
    high = x.astype(jnp.bfloat16)
    low = (x - high.astype(jnp.float32)).astype(jnp.bfloat16)
    return jnp.concatenate([high, low], axis=-1)


def joined_pair(x):
    half = x.shape[-1] // 2
    return x[..., :half].astype(jnp.float32) + x[..., half:].astype(jnp.float32)


def local(
    state0,
    drive,
    cotangent,
    excitatory,
    tile_vals,
    tile_cols,
    tile_count,
    boundary_rows,
    u_factor,
    v_factor,
):
    lanes = lax.axis_size(ROW)
    groups = lax.axis_size("region")
    batch_rows, own_rows = state0.shape
    rank = v_factor.shape[0]
    own_tiles = own_rows // 128
    row_tiles = tile_vals.shape[0]
    chosen = boundary_rows.reshape(-1)
    bound_cols = chosen.shape[0]
    per_lane = own_tiles + bound_cols // 128
    ext_cols = per_lane * 128
    flat_cols = tile_cols.reshape(-1)
    lane_of = flat_cols // per_lane
    at_lane = flat_cols % per_lane
    live_grid = jnp.arange(tile_cols.shape[1], dtype=jnp.int32)[None, :] < tile_count[:, None]
    live_tiles = live_grid.reshape(-1)
    flat_tiles = tile_vals.reshape(-1, 128, 128)
    polarity = (2 * excitatory - 1).astype(jnp.float32)
    state = state0
    saved = []
    for moment in range(STEPS):
        rates = jnp.tanh(state)
        signed = (polarity * rates).astype(jnp.bfloat16)
        outgoing = jnp.take(signed, chosen, axis=1).reshape(batch_rows, groups, -1)
        part_latent = jnp.dot(signed, v_factor.T, preferred_element_type=jnp.float32)
        chunks = jnp.concatenate(
            [
                jnp.moveaxis(outgoing, 1, 0).astype(jnp.float32),
                jnp.broadcast_to(part_latent, (groups, batch_rows, rank)),
            ],
            axis=2,
        )
        got = from_each_region(chunks)
        incoming = jnp.moveaxis(got[:, :, : outgoing.shape[2]], 0, 1).reshape(batch_rows, -1).astype(jnp.bfloat16)
        lane_latent = jnp.sum(got[:, :, outgoing.shape[2] :], axis=0)
        payload = jnp.concatenate([signed, incoming, split_pair(lane_latent)], axis=1)
        copies = jnp.broadcast_to(payload, (lanes, *payload.shape))
        gathered = lax.all_to_all(copies, ROW, 0, 0, tiled=True)
        latent = jnp.sum(joined_pair(gathered[:, :, ext_cols:]), axis=0)
        ext = gathered[:, :, :ext_cols].reshape(lanes, batch_rows, per_lane, 128)
        blocks = ext[lane_of, :, at_lane, :]
        blocks = jnp.where(live_tiles[:, None, None], blocks, jnp.zeros((), blocks.dtype))
        product = jnp.einsum("sbk,sik->bsi", blocks, flat_tiles, preferred_element_type=jnp.float32)
        synaptic = product.reshape(batch_rows, row_tiles, -1, 128).sum(axis=2).reshape(batch_rows, own_rows)
        latent_b = latent.astype(jnp.bfloat16)
        lowrank = jnp.dot(latent_b, u_factor, preferred_element_type=jnp.float32)
        saved.append((rates, signed, latent_b))
        state = state + leak * (-state + synaptic + lowrank + drive.astype(jnp.float32))
    grad_u = jnp.zeros((u_factor.shape[0], own_rows), jnp.float32)
    grad_v = jnp.zeros((v_factor.shape[0], own_rows), jnp.float32)
    adjoint = cotangent
    for moment in reversed(range(STEPS)):
        rates, signed, latent_b = saved[moment]
        scaled_b = (leak * adjoint).astype(jnp.bfloat16)
        part_coeff = jnp.dot(scaled_b, u_factor.T, preferred_element_type=jnp.float32)
        spread = jnp.einsum(
            "bri,rjik->brjk",
            scaled_b.reshape(batch_rows, row_tiles, 128),
            tile_vals,
            preferred_element_type=jnp.float32,
        )
        picks = (flat_cols[None, :] == jnp.arange(lanes * per_lane, dtype=jnp.int32)[:, None]) & live_tiles[None, :]
        picks = picks.astype(jnp.float32).reshape(lanes, per_lane, -1)
        columns = jnp.einsum(
            "lts,bsk->lbtk", picks, spread.reshape(batch_rows, -1, 128), precision=lax.Precision.HIGHEST
        )
        parts = columns.astype(jnp.bfloat16).reshape(lanes, batch_rows, ext_cols)
        coeff_pair = jnp.broadcast_to(split_pair(part_coeff), (lanes, batch_rows, 2 * rank))
        got = lax.all_to_all(jnp.concatenate([parts, coeff_pair], axis=2), ROW, 0, 0, tiled=True)
        summed = jnp.sum(got[:, :, :ext_cols].astype(jnp.float32), axis=0)
        group_coeff = jnp.sum(joined_pair(got[:, :, ext_cols:]), axis=0)
        own_part = summed[:, :own_rows]
        border = summed[:, own_rows:].reshape(batch_rows, groups, -1)
        chunks = jnp.concatenate(
            [jnp.moveaxis(border, 1, 0), jnp.broadcast_to(group_coeff, (groups, batch_rows, rank))], axis=2
        )
        back = from_each_region(chunks)
        returned = jnp.moveaxis(back[:, :, : border.shape[2]], 0, 1).reshape(batch_rows, -1)
        coeffs_b = jnp.sum(back[:, :, border.shape[2] :], axis=0).astype(jnp.bfloat16)
        through = own_part.at[:, chosen].add(returned)
        total_signed = through + jnp.dot(coeffs_b, v_factor, preferred_element_type=jnp.float32)
        grad_u = grad_u + jnp.dot(latent_b.T, scaled_b, preferred_element_type=jnp.float32)
        grad_v = grad_v + jnp.dot(coeffs_b.T, signed, preferred_element_type=jnp.float32)
        adjoint = (1.0 - leak) * adjoint + (1.0 - rates * rates) * polarity * total_signed
    return (state, grad_u, grad_v)


def solution(mesh):
    finer = Mesh(
        mesh.devices.reshape(mesh.shape["region"], 4, 4, 2), ("region", "row_0", "row_1", "row_2")
    )
    in_specs = (
        P(None, REGION_ROW),
        P(None, REGION_ROW),
        P(None, REGION_ROW),
        P(REGION_ROW),
        P(REGION_ROW, None, None, None),
        P(REGION_ROW, None),
        P(REGION_ROW),
        P("region", ROW, None, None),
        P(None, REGION_ROW),
        P(None, REGION_ROW),
    )
    out_specs = (P(None, REGION_ROW), P(None, REGION_ROW), P(None, REGION_ROW))
    return jax.shard_map(local, mesh=finer, in_specs=in_specs, out_specs=out_specs, check_vma=False)
```

```python
import jax
import jax.numpy as jnp
from jax import lax
from jax.sharding import Mesh
from jax.sharding import PartitionSpec as P

STEPS = 4
ROW = ("row_0", "row_1", "row_2")
REGION_ROW = ("region", "row_0", "row_1", "row_2")


leak = 0.5


def from_each_region(chunks):
    return lax.all_to_all(chunks, "region", 0, 0, tiled=True)


def split_pair(x):
    high = x.astype(jnp.bfloat16)
    low = (x - high.astype(jnp.float32)).astype(jnp.bfloat16)
    return jnp.concatenate([high, low], axis=-1)


def joined_pair(x):
    half = x.shape[-1] // 2
    return x[..., :half].astype(jnp.float32) + x[..., half:].astype(jnp.float32)


def padded_slot(x):
    return jnp.pad(x, ((0, 0), (0, 128 - x.shape[1])))[None]


def local(
    state0,
    drive,
    cotangent,
    excitatory,
    tile_vals,
    tile_cols,
    tile_count,
    boundary_rows,
    u_factor,
    v_factor,
):
    lanes = lax.axis_size(ROW)
    groups = lax.axis_size("region")
    batch_rows, own_rows = state0.shape
    rank = v_factor.shape[0]
    own_tiles = own_rows // 128
    row_tiles = tile_vals.shape[0]
    chosen = boundary_rows.reshape(-1)
    bound_cols = chosen.shape[0]
    per_lane = own_tiles + bound_cols // 128
    flat_cols = tile_cols.reshape(-1)
    lane_of = flat_cols // per_lane
    at_lane = flat_cols % per_lane
    live_grid = jnp.arange(tile_cols.shape[1], dtype=jnp.int32)[None, :] < tile_count[:, None]
    live_tiles = live_grid.reshape(-1)
    flat_tiles = tile_vals.reshape(-1, 128, 128)
    polarity = (2 * excitatory - 1).astype(jnp.float32)
    state = state0
    saved = []
    for moment in range(STEPS):
        rates = jnp.tanh(state)
        signed = (polarity * rates).astype(jnp.bfloat16)
        outgoing = jnp.take(signed, chosen, axis=1).reshape(batch_rows, groups, -1)
        part_latent = jnp.dot(signed, v_factor.T, preferred_element_type=jnp.float32)
        chunks = jnp.concatenate(
            [
                jnp.moveaxis(outgoing, 1, 0).astype(jnp.float32),
                jnp.broadcast_to(part_latent, (groups, batch_rows, rank)),
            ],
            axis=2,
        )
        got = from_each_region(chunks)
        incoming = jnp.moveaxis(got[:, :, : outgoing.shape[2]], 0, 1).reshape(batch_rows, -1).astype(jnp.bfloat16)
        lane_latent = jnp.sum(got[:, :, outgoing.shape[2] :], axis=0)
        slots = jnp.concatenate(
            [
                jnp.moveaxis(signed.reshape(batch_rows, own_tiles, 128), 1, 0),
                incoming.reshape(1, batch_rows, -1),
                padded_slot(split_pair(lane_latent)),
            ],
            axis=0,
        )
        copies = jnp.broadcast_to(slots, (lanes, *slots.shape))
        gathered = lax.all_to_all(copies, ROW, 0, 0, tiled=True)
        latent = jnp.sum(joined_pair(gathered[:, per_lane, :, : 2 * rank]), axis=0)
        blocks = gathered[lane_of, at_lane]
        blocks = jnp.where(live_tiles[:, None, None], blocks, jnp.zeros((), blocks.dtype))
        product = jnp.einsum("sbk,sik->bsi", blocks, flat_tiles, preferred_element_type=jnp.float32)
        synaptic = product.reshape(batch_rows, row_tiles, -1, 128).sum(axis=2).reshape(batch_rows, own_rows)
        latent_b = latent.astype(jnp.bfloat16)
        lowrank = jnp.dot(latent_b, u_factor, preferred_element_type=jnp.float32)
        saved.append((rates, signed, latent_b))
        state = state + leak * (-state + synaptic + lowrank + drive.astype(jnp.float32))
    grad_u = jnp.zeros((u_factor.shape[0], own_rows), jnp.float32)
    grad_v = jnp.zeros((v_factor.shape[0], own_rows), jnp.float32)
    adjoint = cotangent
    for moment in reversed(range(STEPS)):
        rates, signed, latent_b = saved[moment]
        scaled_b = (leak * adjoint).astype(jnp.bfloat16)
        part_coeff = jnp.dot(scaled_b, u_factor.T, preferred_element_type=jnp.float32)
        spread = jnp.einsum(
            "bri,rjik->brjk",
            scaled_b.reshape(batch_rows, row_tiles, 128),
            tile_vals,
            preferred_element_type=jnp.float32,
        )
        picks = (flat_cols[None, :] == jnp.arange(lanes * per_lane, dtype=jnp.int32)[:, None]) & live_tiles[None, :]
        picks = picks.astype(jnp.float32).reshape(lanes, per_lane, -1)
        columns = jnp.einsum(
            "lts,bsk->ltbk", picks, spread.reshape(batch_rows, -1, 128), precision=lax.Precision.HIGHEST
        )
        coeff_slot = jnp.broadcast_to(padded_slot(split_pair(part_coeff)), (lanes, 1, batch_rows, 128))
        payload = jnp.concatenate([columns.astype(jnp.bfloat16), coeff_slot], axis=1)
        got = lax.all_to_all(payload, ROW, 0, 0, tiled=True)
        summed = jnp.sum(got[:, :per_lane].astype(jnp.float32), axis=0)
        group_coeff = jnp.sum(joined_pair(got[:, per_lane, :, : 2 * rank]), axis=0)
        own_part = jnp.moveaxis(summed[:own_tiles], 0, 1).reshape(batch_rows, own_rows)
        border = summed[own_tiles:].reshape(batch_rows, groups, -1)
        chunks = jnp.concatenate(
            [jnp.moveaxis(border, 1, 0), jnp.broadcast_to(group_coeff, (groups, batch_rows, rank))], axis=2
        )
        back = from_each_region(chunks)
        returned = jnp.moveaxis(back[:, :, : border.shape[2]], 0, 1).reshape(batch_rows, -1)
        coeffs_b = jnp.sum(back[:, :, border.shape[2] :], axis=0).astype(jnp.bfloat16)
        through = own_part.at[:, chosen].add(returned)
        total_signed = through + jnp.dot(coeffs_b, v_factor, preferred_element_type=jnp.float32)
        grad_u = grad_u + jnp.dot(latent_b.T, scaled_b, preferred_element_type=jnp.float32)
        grad_v = grad_v + jnp.dot(coeffs_b.T, signed, preferred_element_type=jnp.float32)
        adjoint = (1.0 - leak) * adjoint + (1.0 - rates * rates) * polarity * total_signed
    return (state, grad_u, grad_v)


def solution(mesh):
    finer = Mesh(
        mesh.devices.reshape(mesh.shape["region"], 4, 4, 2), ("region", "row_0", "row_1", "row_2")
    )
    in_specs = (
        P(None, REGION_ROW),
        P(None, REGION_ROW),
        P(None, REGION_ROW),
        P(REGION_ROW),
        P(REGION_ROW, None, None, None),
        P(REGION_ROW, None),
        P(REGION_ROW),
        P("region", ROW, None, None),
        P(None, REGION_ROW),
        P(None, REGION_ROW),
    )
    out_specs = (P(None, REGION_ROW), P(None, REGION_ROW), P(None, REGION_ROW))
    return jax.shard_map(local, mesh=finer, in_specs=in_specs, out_specs=out_specs, check_vma=False)
```

```python
import jax
import jax.numpy as jnp
from jax import lax
from jax.sharding import Mesh
from jax.sharding import PartitionSpec as P

STEPS = 4
ROW = ("row_0", "row_1", "row_2")
REGION_ROW = ("region", "row_0", "row_1", "row_2")


leak = 0.5


def from_each_region(chunks):
    return lax.all_to_all(chunks, "region", 0, 0, tiled=True)


def from_each_lane(slots):
    return lax.all_to_all(slots, ROW, 0, 0, tiled=True)


def split_pair(x):
    high = x.astype(jnp.bfloat16)
    low = (x - high.astype(jnp.float32)).astype(jnp.bfloat16)
    return jnp.concatenate([high, low], axis=-1)


def joined_pair(x):
    half = x.shape[-1] // 2
    return x[..., :half].astype(jnp.float32) + x[..., half:].astype(jnp.float32)


def padded_slot(x):
    return jnp.pad(x, ((0, 0), (0, 128 - x.shape[1])))[None]


def local(
    state0,
    drive,
    cotangent,
    excitatory,
    tile_vals,
    tile_cols,
    tile_count,
    boundary_rows,
    u_factor,
    v_factor,
):
    lanes = lax.axis_size(ROW)
    groups = lax.axis_size("region")
    batch_rows, own_rows = state0.shape
    rank = v_factor.shape[0]
    own_tiles = own_rows // 128
    row_tiles = tile_vals.shape[0]
    chosen = boundary_rows.reshape(-1)
    bound_cols = chosen.shape[0]
    per_lane = own_tiles + bound_cols // 128
    slot_count = per_lane + 1
    sent = bound_cols // groups
    region_width = sent + rank
    flat_cols = tile_cols.reshape(-1)
    lane_of = flat_cols // per_lane
    at_lane = flat_cols % per_lane
    live_grid = jnp.arange(tile_cols.shape[1], dtype=jnp.int32)[None, :] < tile_count[:, None]
    live_tiles = live_grid.reshape(-1)
    flat_tiles = tile_vals.reshape(-1, 128, 128)
    picks = (flat_cols[None, :] == jnp.arange(lanes * per_lane, dtype=jnp.int32)[:, None]) & live_tiles[None, :]
    picks = picks.astype(jnp.float32).reshape(lanes, per_lane, -1)
    polarity = (2 * excitatory - 1).astype(jnp.float32)
    drive_f = drive.astype(jnp.float32)

    def forward_start(state):
        rates = jnp.tanh(state)
        signed = (polarity * rates).astype(jnp.bfloat16)
        outgoing = jnp.take(signed, chosen, axis=1).reshape(batch_rows, groups, sent)
        part_latent = jnp.dot(signed, v_factor.T, preferred_element_type=jnp.float32)
        chunks = jnp.concatenate(
            [
                jnp.moveaxis(outgoing, 1, 0).astype(jnp.float32),
                jnp.broadcast_to(part_latent, (groups, batch_rows, rank)),
            ],
            axis=2,
        )
        return rates, signed, chunks

    def forward_middle(signed, got):
        incoming = jnp.moveaxis(got[:, :, :sent], 0, 1).reshape(batch_rows, -1).astype(jnp.bfloat16)
        lane_latent = jnp.sum(got[:, :, sent:], axis=0)
        slots = jnp.concatenate(
            [
                jnp.moveaxis(signed.reshape(batch_rows, own_tiles, 128), 1, 0),
                incoming.reshape(1, batch_rows, -1),
                padded_slot(split_pair(lane_latent)),
            ],
            axis=0,
        )
        return jnp.broadcast_to(slots, (lanes, *slots.shape))

    def forward_end(state, gathered):
        latent = jnp.sum(joined_pair(gathered[:, per_lane, :, : 2 * rank]), axis=0)
        blocks = gathered[lane_of, at_lane]
        blocks = jnp.where(live_tiles[:, None, None], blocks, jnp.zeros((), blocks.dtype))
        product = jnp.einsum("sbk,sik->bsi", blocks, flat_tiles, preferred_element_type=jnp.float32)
        synaptic = product.reshape(batch_rows, row_tiles, -1, 128).sum(axis=2).reshape(batch_rows, own_rows)
        latent_b = latent.astype(jnp.bfloat16)
        lowrank = jnp.dot(latent_b, u_factor, preferred_element_type=jnp.float32)
        return state + leak * (-state + synaptic + lowrank + drive_f), latent_b

    def adjoint_start(adjoint):
        scaled_b = (leak * adjoint).astype(jnp.bfloat16)
        part_coeff = jnp.dot(scaled_b, u_factor.T, preferred_element_type=jnp.float32)
        spread = jnp.einsum(
            "bri,rjik->brjk",
            scaled_b.reshape(batch_rows, row_tiles, 128),
            tile_vals,
            preferred_element_type=jnp.float32,
        )
        columns = jnp.einsum(
            "lts,bsk->ltbk", picks, spread.reshape(batch_rows, -1, 128), precision=lax.Precision.HIGHEST
        )
        coeff_slot = jnp.broadcast_to(padded_slot(split_pair(part_coeff)), (lanes, 1, batch_rows, 128))
        return scaled_b, jnp.concatenate([columns.astype(jnp.bfloat16), coeff_slot], axis=1)

    def adjoint_middle(got):
        summed = jnp.sum(got[:, :per_lane].astype(jnp.float32), axis=0)
        group_coeff = jnp.sum(joined_pair(got[:, per_lane, :, : 2 * rank]), axis=0)
        own_part = jnp.moveaxis(summed[:own_tiles], 0, 1).reshape(batch_rows, own_rows)
        border = summed[own_tiles:].reshape(batch_rows, groups, sent)
        chunks = jnp.concatenate(
            [jnp.moveaxis(border, 1, 0), jnp.broadcast_to(group_coeff, (groups, batch_rows, rank))], axis=2
        )
        return own_part, chunks

    def adjoint_end(adjoint, own_part, back, rates):
        returned = jnp.moveaxis(back[:, :, :sent], 0, 1).reshape(batch_rows, -1)
        coeffs_b = jnp.sum(back[:, :, sent:], axis=0).astype(jnp.bfloat16)
        through = own_part.at[:, chosen].add(returned)
        total_signed = through + jnp.dot(coeffs_b, v_factor, preferred_element_type=jnp.float32)
        adjoint = (1.0 - leak) * adjoint + (1.0 - rates * rates) * polarity * total_signed
        return adjoint, coeffs_b

    def both_lanes(first, second):
        got = from_each_lane(jnp.concatenate([first, second], axis=1))
        return got[:, :slot_count], got[:, slot_count:]

    def both_regions(first, second):
        got = from_each_region(jnp.concatenate([first, second], axis=2))
        return got[:, :, :region_width], got[:, :, region_width:]

    rates_of, signed_of, latent_of, scaled_of, coeffs_of = {}, {}, {}, {}, {}
    state = state0
    rates_of[0], signed_of[0], chunks = forward_start(state)
    got = from_each_region(chunks)
    scaled_of[3], lane_parts = adjoint_start(cotangent)
    gathered, got_last = both_lanes(forward_middle(signed_of[0], got), lane_parts)
    state, latent_of[0] = forward_end(state, gathered)
    own_last, chunks_last = adjoint_middle(got_last)
    rates_of[1], signed_of[1], chunks = forward_start(state)
    got, back_last = both_regions(chunks, chunks_last)
    gathered = from_each_lane(forward_middle(signed_of[1], got))
    state, latent_of[1] = forward_end(state, gathered)
    rates_of[2], signed_of[2], chunks = forward_start(state)
    got = from_each_region(chunks)
    gathered = from_each_lane(forward_middle(signed_of[2], got))
    state, latent_of[2] = forward_end(state, gathered)
    rates_of[3], signed_of[3], chunks_f3 = forward_start(state)
    adjoint, coeffs_of[3] = adjoint_end(cotangent, own_last, back_last, rates_of[3])
    scaled_of[2], lane_parts = adjoint_start(adjoint)
    own_part, chunks = adjoint_middle(from_each_lane(lane_parts))
    got_f3, back = both_regions(chunks_f3, chunks)
    adjoint, coeffs_of[2] = adjoint_end(adjoint, own_part, back, rates_of[2])
    scaled_of[1], lane_parts = adjoint_start(adjoint)
    got, gathered_f3 = both_lanes(lane_parts, forward_middle(signed_of[3], got_f3))
    final_state, latent_of[3] = forward_end(state, gathered_f3)
    own_part, chunks = adjoint_middle(got)
    adjoint, coeffs_of[1] = adjoint_end(adjoint, own_part, from_each_region(chunks), rates_of[1])
    scaled_of[0], lane_parts = adjoint_start(adjoint)
    own_part, chunks = adjoint_middle(from_each_lane(lane_parts))
    adjoint, coeffs_of[0] = adjoint_end(adjoint, own_part, from_each_region(chunks), rates_of[0])
    grad_u = jnp.zeros((rank, own_rows), jnp.float32)
    grad_v = jnp.zeros((rank, own_rows), jnp.float32)
    for moment in reversed(range(STEPS)):
        grad_u = grad_u + jnp.dot(latent_of[moment].T, scaled_of[moment], preferred_element_type=jnp.float32)
        grad_v = grad_v + jnp.dot(coeffs_of[moment].T, signed_of[moment], preferred_element_type=jnp.float32)
    return (final_state, grad_u, grad_v)


def solution(mesh):
    finer = Mesh(
        mesh.devices.reshape(mesh.shape["region"], 4, 4, 2), ("region", "row_0", "row_1", "row_2")
    )
    in_specs = (
        P(None, REGION_ROW),
        P(None, REGION_ROW),
        P(None, REGION_ROW),
        P(REGION_ROW),
        P(REGION_ROW, None, None, None),
        P(REGION_ROW, None),
        P(REGION_ROW),
        P("region", ROW, None, None),
        P(None, REGION_ROW),
        P(None, REGION_ROW),
    )
    out_specs = (P(None, REGION_ROW), P(None, REGION_ROW), P(None, REGION_ROW))
    return jax.shard_map(local, mesh=finer, in_specs=in_specs, out_specs=out_specs, check_vma=False)
```

```python
import jax
import jax.numpy as jnp
from jax import lax
from jax.sharding import Mesh
from jax.sharding import PartitionSpec as P

STEPS = 4
ROW = ("row_0", "row_1", "row_2")
REGION_ROW = ("region", "row_0", "row_1", "row_2")


leak = 0.5


def from_each_region(chunks):
    return lax.all_to_all(chunks, "region", 0, 0, tiled=True)


def from_each_lane(slots):
    return lax.all_to_all(slots, ROW, 0, 0, tiled=True)


def split_pair(x):
    high = x.astype(jnp.bfloat16)
    low = (x - high.astype(jnp.float32)).astype(jnp.bfloat16)
    return jnp.concatenate([high, low], axis=-1)


def joined_pair(x):
    half = x.shape[-1] // 2
    return x[..., :half].astype(jnp.float32) + x[..., half:].astype(jnp.float32)


def local(
    state0,
    drive,
    cotangent,
    excitatory,
    tile_vals,
    tile_cols,
    tile_count,
    boundary_rows,
    u_factor,
    v_factor,
):
    lanes = lax.axis_size(ROW)
    groups = lax.axis_size("region")
    batch_rows, own_rows = state0.shape
    rank = v_factor.shape[0]
    own_tiles = own_rows // 128
    row_tiles = tile_vals.shape[0]
    chosen = boundary_rows.reshape(-1)
    bound_cols = chosen.shape[0]
    per_lane = own_tiles + bound_cols // 128
    tile_rows = per_lane * batch_rows
    sent = bound_cols // groups
    region_width = sent + rank
    flat_cols = tile_cols.reshape(-1)
    lane_of = flat_cols // per_lane
    at_lane = flat_cols % per_lane
    live_grid = jnp.arange(tile_cols.shape[1], dtype=jnp.int32)[None, :] < tile_count[:, None]
    live_tiles = live_grid.reshape(-1)
    flat_tiles = tile_vals.reshape(-1, 128, 128)
    picks = (flat_cols[None, :] == jnp.arange(lanes * per_lane, dtype=jnp.int32)[:, None]) & live_tiles[None, :]
    picks = picks.astype(jnp.float32).reshape(lanes, per_lane, -1)
    polarity = (2 * excitatory - 1).astype(jnp.float32)
    drive_f = drive.astype(jnp.float32)

    def forward_start(state):
        rates = jnp.tanh(state)
        signed = (polarity * rates).astype(jnp.bfloat16)
        outgoing = jnp.take(signed, chosen, axis=1).reshape(batch_rows, groups, sent)
        part_latent = jnp.dot(signed, v_factor.T, preferred_element_type=jnp.float32)
        chunks = jnp.concatenate(
            [
                jnp.moveaxis(outgoing, 1, 0).astype(jnp.float32),
                jnp.broadcast_to(part_latent, (groups, batch_rows, rank)),
            ],
            axis=2,
        )
        return rates, signed, chunks

    def forward_middle(signed, got):
        incoming = jnp.moveaxis(got[:, :, :sent], 0, 1).reshape(batch_rows, -1).astype(jnp.bfloat16)
        lane_latent = jnp.sum(got[:, :, sent:], axis=0)
        slots = jnp.concatenate(
            [
                jnp.moveaxis(signed.reshape(batch_rows, own_tiles, 128), 1, 0).reshape(-1, 128),
                incoming.reshape(batch_rows, -1),
                split_pair(lane_latent).reshape(-1, 128),
            ],
            axis=0,
        )
        return jnp.broadcast_to(slots, (lanes, *slots.shape))

    def forward_end(state, gathered):
        latent = jnp.sum(joined_pair(gathered[:, tile_rows:].reshape(lanes, batch_rows, 2 * rank)), axis=0)
        blocks = gathered[:, :tile_rows].reshape(lanes, per_lane, batch_rows, 128)[lane_of, at_lane]
        blocks = jnp.where(live_tiles[:, None, None], blocks, jnp.zeros((), blocks.dtype))
        product = jnp.einsum("sbk,sik->bsi", blocks, flat_tiles, preferred_element_type=jnp.float32)
        synaptic = product.reshape(batch_rows, row_tiles, -1, 128).sum(axis=2).reshape(batch_rows, own_rows)
        latent_b = latent.astype(jnp.bfloat16)
        lowrank = jnp.dot(latent_b, u_factor, preferred_element_type=jnp.float32)
        return state + leak * (-state + synaptic + lowrank + drive_f), latent_b

    def adjoint_start(adjoint):
        scaled_b = (leak * adjoint).astype(jnp.bfloat16)
        part_coeff = jnp.dot(scaled_b, u_factor.T, preferred_element_type=jnp.float32)
        spread = jnp.einsum(
            "bri,rjik->brjk",
            scaled_b.reshape(batch_rows, row_tiles, 128),
            tile_vals,
            preferred_element_type=jnp.float32,
        )
        columns = jnp.einsum(
            "lts,bsk->ltbk", picks, spread.reshape(batch_rows, -1, 128), precision=lax.Precision.HIGHEST
        )
        pair_rows = split_pair(part_coeff).reshape(-1, 128)
        coeff_rows = jnp.broadcast_to(pair_rows, (lanes, *pair_rows.shape))
        tiles_rows = columns.astype(jnp.bfloat16).reshape(lanes, tile_rows, 128)
        return scaled_b, jnp.concatenate([tiles_rows, coeff_rows], axis=1)

    def adjoint_middle(got):
        summed = jnp.sum(got[:, :tile_rows].astype(jnp.float32), axis=0).reshape(per_lane, batch_rows, 128)
        group_coeff = jnp.sum(joined_pair(got[:, tile_rows:].reshape(lanes, batch_rows, 2 * rank)), axis=0)
        own_part = jnp.moveaxis(summed[:own_tiles], 0, 1).reshape(batch_rows, own_rows)
        border = summed[own_tiles:].reshape(batch_rows, groups, sent)
        chunks = jnp.concatenate(
            [jnp.moveaxis(border, 1, 0), jnp.broadcast_to(group_coeff, (groups, batch_rows, rank))], axis=2
        )
        return own_part, chunks

    def adjoint_end(adjoint, own_part, back, rates):
        returned = jnp.moveaxis(back[:, :, :sent], 0, 1).reshape(batch_rows, -1)
        coeffs_b = jnp.sum(back[:, :, sent:], axis=0).astype(jnp.bfloat16)
        through = own_part.at[:, chosen].add(returned)
        total_signed = through + jnp.dot(coeffs_b, v_factor, preferred_element_type=jnp.float32)
        adjoint = (1.0 - leak) * adjoint + (1.0 - rates * rates) * polarity * total_signed
        return adjoint, coeffs_b

    def both_regions(first, second):
        got = from_each_region(jnp.concatenate([first, second], axis=2))
        return got[:, :, :region_width], got[:, :, region_width:]

    rates_of, signed_of, latent_of, scaled_of, coeffs_of = {}, {}, {}, {}, {}
    state = state0
    rates_of[0], signed_of[0], chunks = forward_start(state)
    got = from_each_region(chunks)
    scaled_of[3], lane_parts = adjoint_start(cotangent)
    got_last = from_each_lane(lane_parts)
    gathered = from_each_lane(forward_middle(signed_of[0], got))
    state, latent_of[0] = forward_end(state, gathered)
    own_last, chunks_last = adjoint_middle(got_last)
    rates_of[1], signed_of[1], chunks = forward_start(state)
    got, back_last = both_regions(chunks, chunks_last)
    gathered = from_each_lane(forward_middle(signed_of[1], got))
    state, latent_of[1] = forward_end(state, gathered)
    rates_of[2], signed_of[2], chunks = forward_start(state)
    got = from_each_region(chunks)
    gathered = from_each_lane(forward_middle(signed_of[2], got))
    state, latent_of[2] = forward_end(state, gathered)
    rates_of[3], signed_of[3], chunks_f3 = forward_start(state)
    adjoint, coeffs_of[3] = adjoint_end(cotangent, own_last, back_last, rates_of[3])
    scaled_of[2], lane_parts = adjoint_start(adjoint)
    own_part, chunks = adjoint_middle(from_each_lane(lane_parts))
    got_f3, back = both_regions(chunks_f3, chunks)
    adjoint, coeffs_of[2] = adjoint_end(adjoint, own_part, back, rates_of[2])
    scaled_of[1], lane_parts = adjoint_start(adjoint)
    gathered_f3 = from_each_lane(forward_middle(signed_of[3], got_f3))
    got = from_each_lane(lane_parts)
    final_state, latent_of[3] = forward_end(state, gathered_f3)
    own_part, chunks = adjoint_middle(got)
    adjoint, coeffs_of[1] = adjoint_end(adjoint, own_part, from_each_region(chunks), rates_of[1])
    scaled_of[0], lane_parts = adjoint_start(adjoint)
    own_part, chunks = adjoint_middle(from_each_lane(lane_parts))
    adjoint, coeffs_of[0] = adjoint_end(adjoint, own_part, from_each_region(chunks), rates_of[0])
    grad_u = jnp.zeros((rank, own_rows), jnp.float32)
    grad_v = jnp.zeros((rank, own_rows), jnp.float32)
    for moment in reversed(range(STEPS)):
        grad_u = grad_u + jnp.dot(latent_of[moment].T, scaled_of[moment], preferred_element_type=jnp.float32)
        grad_v = grad_v + jnp.dot(coeffs_of[moment].T, signed_of[moment], preferred_element_type=jnp.float32)
    return (final_state, grad_u, grad_v)


def solution(mesh):
    finer = Mesh(
        mesh.devices.reshape(mesh.shape["region"], 4, 4, 2), ("region", "row_0", "row_1", "row_2")
    )
    in_specs = (
        P(None, REGION_ROW),
        P(None, REGION_ROW),
        P(None, REGION_ROW),
        P(REGION_ROW),
        P(REGION_ROW, None, None, None),
        P(REGION_ROW, None),
        P(REGION_ROW),
        P("region", ROW, None, None),
        P(None, REGION_ROW),
        P(None, REGION_ROW),
    )
    out_specs = (P(None, REGION_ROW), P(None, REGION_ROW), P(None, REGION_ROW))
    return jax.shard_map(local, mesh=finer, in_specs=in_specs, out_specs=out_specs, check_vma=False)
```

```python
import jax
import jax.numpy as jnp
from jax import lax
from jax.sharding import Mesh
from jax.sharding import PartitionSpec as P

STEPS = 4
ROW = ("row_0", "row_1", "row_2")
REGION_ROW = ("region", "row_0", "row_1", "row_2")


leak = 0.5


def from_each_region(chunks):
    return lax.all_to_all(chunks, "region", 0, 0, tiled=True)


def from_each_lane(slots):
    return lax.all_to_all(slots, ROW, 0, 0, tiled=True)


def from_every_lane(slots):
    chips = ROW[:-1]
    copies = jnp.broadcast_to(slots, (lax.axis_size(chips), *slots.shape))
    mine = lax.all_to_all(copies, chips, 0, 0, tiled=True)
    sibling = lax.ppermute(mine, ROW[-1], [(0, 1), (1, 0)])
    return jnp.stack([mine, sibling])


def split_pair(x):
    high = x.astype(jnp.bfloat16)
    low = (x - high.astype(jnp.float32)).astype(jnp.bfloat16)
    return jnp.concatenate([high, low], axis=-1)


def joined_pair(x):
    half = x.shape[-1] // 2
    return x[..., :half].astype(jnp.float32) + x[..., half:].astype(jnp.float32)


def local(
    state0,
    drive,
    cotangent,
    excitatory,
    tile_vals,
    tile_cols,
    tile_count,
    boundary_rows,
    u_factor,
    v_factor,
):
    lanes = lax.axis_size(ROW)
    groups = lax.axis_size("region")
    batch_rows, own_rows = state0.shape
    rank = v_factor.shape[0]
    own_tiles = own_rows // 128
    row_tiles = tile_vals.shape[0]
    chosen = boundary_rows.reshape(-1)
    bound_cols = chosen.shape[0]
    per_lane = own_tiles + bound_cols // 128
    tile_rows = per_lane * batch_rows
    sent = bound_cols // groups
    region_width = sent + rank
    flat_cols = tile_cols.reshape(-1)
    lane_of = flat_cols // per_lane
    cores = lax.axis_size(ROW[-1])
    side_of = (lane_of % cores != lax.axis_index(ROW[-1])).astype(jnp.int32)
    chip_of = lane_of // cores
    at_lane = flat_cols % per_lane
    live_grid = jnp.arange(tile_cols.shape[1], dtype=jnp.int32)[None, :] < tile_count[:, None]
    live_tiles = live_grid.reshape(-1)
    flat_tiles = tile_vals.reshape(-1, 128, 128)
    picks = (flat_cols[None, :] == jnp.arange(lanes * per_lane, dtype=jnp.int32)[:, None]) & live_tiles[None, :]
    picks = picks.astype(jnp.float32).reshape(lanes, per_lane, -1)
    polarity = (2 * excitatory - 1).astype(jnp.float32)
    drive_f = drive.astype(jnp.float32)

    def forward_start(state):
        rates = jnp.tanh(state)
        signed = (polarity * rates).astype(jnp.bfloat16)
        outgoing = jnp.take(signed, chosen, axis=1).reshape(batch_rows, groups, sent)
        part_latent = jnp.dot(signed, v_factor.T, preferred_element_type=jnp.float32)
        chunks = jnp.concatenate(
            [
                jnp.moveaxis(outgoing, 1, 0).astype(jnp.float32),
                jnp.broadcast_to(part_latent, (groups, batch_rows, rank)),
            ],
            axis=2,
        )
        return rates, signed, chunks

    def forward_middle(signed, got):
        incoming = jnp.moveaxis(got[:, :, :sent], 0, 1).reshape(batch_rows, -1).astype(jnp.bfloat16)
        lane_latent = jnp.sum(got[:, :, sent:], axis=0)
        slots = jnp.concatenate(
            [
                jnp.moveaxis(signed.reshape(batch_rows, own_tiles, 128), 1, 0).reshape(-1, 128),
                incoming.reshape(batch_rows, -1),
                split_pair(lane_latent).reshape(-1, 128),
            ],
            axis=0,
        )
        return slots

    def forward_end(state, gathered):
        pair_rows = gathered[:, :, tile_rows:].reshape(lanes, batch_rows, 2 * rank)
        latent = jnp.sum(joined_pair(pair_rows), axis=0)
        pick = lambda side, chip, tile: lax.dynamic_slice(gathered, (side, chip, tile * batch_rows, 0), (1, 1, batch_rows, 128))
        blocks = jax.vmap(pick)(side_of, chip_of, at_lane).reshape(-1, batch_rows, 128)
        blocks = jnp.where(live_tiles[:, None, None], blocks, jnp.zeros((), blocks.dtype))
        product = jnp.einsum("sbk,sik->bsi", blocks, flat_tiles, preferred_element_type=jnp.float32)
        synaptic = product.reshape(batch_rows, row_tiles, -1, 128).sum(axis=2).reshape(batch_rows, own_rows)
        latent_b = latent.astype(jnp.bfloat16)
        lowrank = jnp.dot(latent_b, u_factor, preferred_element_type=jnp.float32)
        return state + leak * (-state + synaptic + lowrank + drive_f), latent_b

    def adjoint_start(adjoint):
        scaled_b = (leak * adjoint).astype(jnp.bfloat16)
        part_coeff = jnp.dot(scaled_b, u_factor.T, preferred_element_type=jnp.float32)
        spread = jnp.einsum(
            "bri,rjik->brjk",
            scaled_b.reshape(batch_rows, row_tiles, 128),
            tile_vals,
            preferred_element_type=jnp.float32,
        )
        columns = jnp.einsum(
            "lts,bsk->ltbk", picks, spread.reshape(batch_rows, -1, 128), precision=lax.Precision.HIGHEST
        )
        pair_rows = split_pair(part_coeff).reshape(-1, 128)
        coeff_rows = jnp.broadcast_to(pair_rows, (lanes, *pair_rows.shape))
        tiles_rows = columns.astype(jnp.bfloat16).reshape(lanes, tile_rows, 128)
        return scaled_b, jnp.concatenate([tiles_rows, coeff_rows], axis=1)

    def adjoint_middle(got):
        summed = jnp.sum(got[:, :tile_rows].astype(jnp.float32), axis=0).reshape(per_lane, batch_rows, 128)
        group_coeff = jnp.sum(joined_pair(got[:, tile_rows:].reshape(lanes, batch_rows, 2 * rank)), axis=0)
        own_part = jnp.moveaxis(summed[:own_tiles], 0, 1).reshape(batch_rows, own_rows)
        border = summed[own_tiles:].reshape(batch_rows, groups, sent)
        chunks = jnp.concatenate(
            [jnp.moveaxis(border, 1, 0), jnp.broadcast_to(group_coeff, (groups, batch_rows, rank))], axis=2
        )
        return own_part, chunks

    def adjoint_end(adjoint, own_part, back, rates):
        returned = jnp.moveaxis(back[:, :, :sent], 0, 1).reshape(batch_rows, -1)
        coeffs_b = jnp.sum(back[:, :, sent:], axis=0).astype(jnp.bfloat16)
        through = own_part.at[:, chosen].add(returned)
        total_signed = through + jnp.dot(coeffs_b, v_factor, preferred_element_type=jnp.float32)
        adjoint = (1.0 - leak) * adjoint + (1.0 - rates * rates) * polarity * total_signed
        return adjoint, coeffs_b

    def both_regions(first, second):
        got = from_each_region(jnp.concatenate([first, second], axis=2))
        return got[:, :, :region_width], got[:, :, region_width:]

    rates_of, signed_of, latent_of, scaled_of, coeffs_of = {}, {}, {}, {}, {}
    state = state0
    rates_of[0], signed_of[0], chunks = forward_start(state)
    got = from_each_region(chunks)
    scaled_of[3], lane_parts = adjoint_start(cotangent)
    got_last = from_each_lane(lane_parts)
    gathered = from_every_lane(forward_middle(signed_of[0], got))
    state, latent_of[0] = forward_end(state, gathered)
    own_last, chunks_last = adjoint_middle(got_last)
    rates_of[1], signed_of[1], chunks = forward_start(state)
    got, back_last = both_regions(chunks, chunks_last)
    gathered = from_every_lane(forward_middle(signed_of[1], got))
    state, latent_of[1] = forward_end(state, gathered)
    rates_of[2], signed_of[2], chunks = forward_start(state)
    got = from_each_region(chunks)
    gathered = from_every_lane(forward_middle(signed_of[2], got))
    state, latent_of[2] = forward_end(state, gathered)
    rates_of[3], signed_of[3], chunks_f3 = forward_start(state)
    adjoint, coeffs_of[3] = adjoint_end(cotangent, own_last, back_last, rates_of[3])
    scaled_of[2], lane_parts = adjoint_start(adjoint)
    own_part, chunks = adjoint_middle(from_each_lane(lane_parts))
    got_f3, back = both_regions(chunks_f3, chunks)
    adjoint, coeffs_of[2] = adjoint_end(adjoint, own_part, back, rates_of[2])
    scaled_of[1], lane_parts = adjoint_start(adjoint)
    gathered_f3 = from_every_lane(forward_middle(signed_of[3], got_f3))
    got = from_each_lane(lane_parts)
    final_state, latent_of[3] = forward_end(state, gathered_f3)
    own_part, chunks = adjoint_middle(got)
    adjoint, coeffs_of[1] = adjoint_end(adjoint, own_part, from_each_region(chunks), rates_of[1])
    scaled_of[0], lane_parts = adjoint_start(adjoint)
    own_part, chunks = adjoint_middle(from_each_lane(lane_parts))
    adjoint, coeffs_of[0] = adjoint_end(adjoint, own_part, from_each_region(chunks), rates_of[0])
    grad_u = jnp.zeros((rank, own_rows), jnp.float32)
    grad_v = jnp.zeros((rank, own_rows), jnp.float32)
    for moment in reversed(range(STEPS)):
        grad_u = grad_u + jnp.dot(latent_of[moment].T, scaled_of[moment], preferred_element_type=jnp.float32)
        grad_v = grad_v + jnp.dot(coeffs_of[moment].T, signed_of[moment], preferred_element_type=jnp.float32)
    return (final_state, grad_u, grad_v)


def solution(mesh):
    finer = Mesh(
        mesh.devices.reshape(mesh.shape["region"], 4, 4, 2), ("region", "row_0", "row_1", "row_2")
    )
    in_specs = (
        P(None, REGION_ROW),
        P(None, REGION_ROW),
        P(None, REGION_ROW),
        P(REGION_ROW),
        P(REGION_ROW, None, None, None),
        P(REGION_ROW, None),
        P(REGION_ROW),
        P("region", ROW, None, None),
        P(None, REGION_ROW),
        P(None, REGION_ROW),
    )
    out_specs = (P(None, REGION_ROW), P(None, REGION_ROW), P(None, REGION_ROW))
    return jax.shard_map(local, mesh=finer, in_specs=in_specs, out_specs=out_specs, check_vma=False)
```

```python
import jax
import jax.numpy as jnp
from jax import lax
from jax.sharding import Mesh
from jax.sharding import PartitionSpec as P

STEPS = 4
ROW = ("row_0", "row_1", "row_2")
REGION_ROW = ("region", "row_0", "row_1", "row_2")


leak = 0.5


def from_each_region(chunks):
    return lax.all_to_all(chunks, "region", 0, 0, tiled=True)


def from_each_lane(slots):
    return lax.all_to_all(slots, ROW, 0, 0, tiled=True)


def from_every_lane(slots):
    chips = ROW[:-1]
    copies = jnp.broadcast_to(slots, (lax.axis_size(chips), *slots.shape))
    mine = lax.all_to_all(copies, chips, 0, 0, tiled=True)
    sibling = lax.ppermute(mine, ROW[-1], [(0, 1), (1, 0)])
    return jnp.stack([mine, sibling])


def split_pair(x):
    high = x.astype(jnp.bfloat16)
    low = (x - high.astype(jnp.float32)).astype(jnp.bfloat16)
    return jnp.concatenate([high, low], axis=-1)


def joined_pair(x):
    half = x.shape[-1] // 2
    return x[..., :half].astype(jnp.float32) + x[..., half:].astype(jnp.float32)


def local(
    state0,
    drive,
    cotangent,
    excitatory,
    tile_vals,
    tile_cols,
    tile_count,
    boundary_rows,
    u_factor,
    v_factor,
):
    lanes = lax.axis_size(ROW)
    groups = lax.axis_size("region")
    batch_rows, own_rows = state0.shape
    rank = v_factor.shape[0]
    own_tiles = own_rows // 128
    row_tiles = tile_vals.shape[0]
    chosen = boundary_rows.reshape(-1)
    bound_cols = chosen.shape[0]
    per_lane = own_tiles + bound_cols // 128
    tile_rows = per_lane * batch_rows
    sent = bound_cols // groups
    region_width = sent + rank
    flat_cols = tile_cols.reshape(-1)
    lane_of = flat_cols // per_lane
    cores = lax.axis_size(ROW[-1])
    side_of = (lane_of % cores != lax.axis_index(ROW[-1])).astype(jnp.int32)
    chip_of = lane_of // cores
    at_lane = flat_cols % per_lane
    live_grid = jnp.arange(tile_cols.shape[1], dtype=jnp.int32)[None, :] < tile_count[:, None]
    live_tiles = live_grid.reshape(-1)
    picks = (flat_cols[None, :] == jnp.arange(lanes * per_lane, dtype=jnp.int32)[:, None]) & live_tiles[None, :]
    picks = picks.astype(jnp.float32).reshape(lanes, per_lane, -1)
    half_rows = 16
    halves = batch_rows // half_rows
    payload_rows = tile_rows + batch_rows * 2 * rank // 128
    block_of = at_lane[:, None] * halves + jnp.arange(halves, dtype=jnp.int32)[None, :]
    picks_fwd = (
        (jnp.arange(cores, dtype=jnp.int32)[None, None, :, None, None] == side_of[:, None, None, None, None])
        & (jnp.arange(lanes // cores, dtype=jnp.int32)[None, None, None, :, None] == chip_of[:, None, None, None, None])
        & (jnp.arange(payload_rows // half_rows, dtype=jnp.int32)[None, None, None, None, :] == block_of[:, :, None, None, None])
        & live_tiles[:, None, None, None, None]
    ).astype(jnp.bfloat16)
    polarity = (2 * excitatory - 1).astype(jnp.float32)
    drive_f = drive.astype(jnp.float32)

    def forward_start(state):
        rates = jnp.tanh(state)
        signed = (polarity * rates).astype(jnp.bfloat16)
        outgoing = jnp.take(signed, chosen, axis=1).reshape(batch_rows, groups, sent)
        part_latent = jnp.dot(signed, v_factor.T, preferred_element_type=jnp.float32)
        chunks = jnp.concatenate(
            [
                jnp.moveaxis(outgoing, 1, 0).astype(jnp.float32),
                jnp.broadcast_to(part_latent, (groups, batch_rows, rank)),
            ],
            axis=2,
        )
        return rates, signed, chunks

    def forward_middle(signed, got):
        incoming = jnp.moveaxis(got[:, :, :sent], 0, 1).reshape(batch_rows, -1).astype(jnp.bfloat16)
        lane_latent = jnp.sum(got[:, :, sent:], axis=0)
        slots = jnp.concatenate(
            [
                jnp.moveaxis(signed.reshape(batch_rows, own_tiles, 128), 1, 0).reshape(-1, 128),
                incoming.reshape(batch_rows, -1),
                split_pair(lane_latent).reshape(-1, 128),
            ],
            axis=0,
        )
        return slots

    def forward_end(state, gathered):
        pair_rows = gathered[:, :, tile_rows:].reshape(lanes, batch_rows, 2 * rank)
        latent = jnp.sum(joined_pair(pair_rows), axis=0)
        stacked = gathered.reshape(*gathered.shape[:2], -1, half_rows, 128)
        blocks = jnp.einsum("shpcm,pcmrk->shrk", picks_fwd, stacked, preferred_element_type=jnp.bfloat16)
        blocks = blocks.reshape(row_tiles, -1, batch_rows, 128)
        synaptic = jnp.einsum("qjbk,qjik->bqi", blocks, tile_vals, preferred_element_type=jnp.float32)
        synaptic = synaptic.reshape(batch_rows, own_rows)
        latent_b = latent.astype(jnp.bfloat16)
        lowrank = jnp.dot(latent_b, u_factor, preferred_element_type=jnp.float32)
        return state + leak * (-state + synaptic + lowrank + drive_f), latent_b

    def adjoint_start(adjoint):
        scaled_b = (leak * adjoint).astype(jnp.bfloat16)
        part_coeff = jnp.dot(scaled_b, u_factor.T, preferred_element_type=jnp.float32)
        spread = jnp.einsum(
            "bri,rjik->brjk",
            scaled_b.reshape(batch_rows, row_tiles, 128),
            tile_vals,
            preferred_element_type=jnp.float32,
        )
        columns = jnp.einsum(
            "lts,bsk->ltbk", picks, spread.reshape(batch_rows, -1, 128), precision=lax.Precision.HIGHEST
        )
        pair_rows = split_pair(part_coeff).reshape(-1, 128)
        coeff_rows = jnp.broadcast_to(pair_rows, (lanes, *pair_rows.shape))
        tiles_rows = columns.astype(jnp.bfloat16).reshape(lanes, tile_rows, 128)
        return scaled_b, jnp.concatenate([tiles_rows, coeff_rows], axis=1)

    def adjoint_middle(got):
        summed = jnp.sum(got[:, :tile_rows].astype(jnp.float32), axis=0).reshape(per_lane, batch_rows, 128)
        group_coeff = jnp.sum(joined_pair(got[:, tile_rows:].reshape(lanes, batch_rows, 2 * rank)), axis=0)
        own_part = jnp.moveaxis(summed[:own_tiles], 0, 1).reshape(batch_rows, own_rows)
        border = summed[own_tiles:].reshape(batch_rows, groups, sent)
        chunks = jnp.concatenate(
            [jnp.moveaxis(border, 1, 0), jnp.broadcast_to(group_coeff, (groups, batch_rows, rank))], axis=2
        )
        return own_part, chunks

    def adjoint_end(adjoint, own_part, back, rates):
        returned = jnp.moveaxis(back[:, :, :sent], 0, 1).reshape(batch_rows, -1)
        coeffs_b = jnp.sum(back[:, :, sent:], axis=0).astype(jnp.bfloat16)
        through = own_part.at[:, chosen].add(returned)
        total_signed = through + jnp.dot(coeffs_b, v_factor, preferred_element_type=jnp.float32)
        adjoint = (1.0 - leak) * adjoint + (1.0 - rates * rates) * polarity * total_signed
        return adjoint, coeffs_b

    def both_regions(first, second):
        got = from_each_region(jnp.concatenate([first, second], axis=2))
        return got[:, :, :region_width], got[:, :, region_width:]

    rates_of, signed_of, latent_of, scaled_of, coeffs_of = {}, {}, {}, {}, {}
    state = state0
    rates_of[0], signed_of[0], chunks = forward_start(state)
    got = from_each_region(chunks)
    scaled_of[3], lane_parts = adjoint_start(cotangent)
    got_last = from_each_lane(lane_parts)
    gathered = from_every_lane(forward_middle(signed_of[0], got))
    state, latent_of[0] = forward_end(state, gathered)
    own_last, chunks_last = adjoint_middle(got_last)
    rates_of[1], signed_of[1], chunks = forward_start(state)
    got, back_last = both_regions(chunks, chunks_last)
    gathered = from_every_lane(forward_middle(signed_of[1], got))
    state, latent_of[1] = forward_end(state, gathered)
    rates_of[2], signed_of[2], chunks = forward_start(state)
    got = from_each_region(chunks)
    gathered = from_every_lane(forward_middle(signed_of[2], got))
    state, latent_of[2] = forward_end(state, gathered)
    rates_of[3], signed_of[3], chunks_f3 = forward_start(state)
    adjoint, coeffs_of[3] = adjoint_end(cotangent, own_last, back_last, rates_of[3])
    scaled_of[2], lane_parts = adjoint_start(adjoint)
    own_part, chunks = adjoint_middle(from_each_lane(lane_parts))
    got_f3, back = both_regions(chunks_f3, chunks)
    adjoint, coeffs_of[2] = adjoint_end(adjoint, own_part, back, rates_of[2])
    scaled_of[1], lane_parts = adjoint_start(adjoint)
    gathered_f3 = from_every_lane(forward_middle(signed_of[3], got_f3))
    got = from_each_lane(lane_parts)
    final_state, latent_of[3] = forward_end(state, gathered_f3)
    own_part, chunks = adjoint_middle(got)
    adjoint, coeffs_of[1] = adjoint_end(adjoint, own_part, from_each_region(chunks), rates_of[1])
    scaled_of[0], lane_parts = adjoint_start(adjoint)
    own_part, chunks = adjoint_middle(from_each_lane(lane_parts))
    adjoint, coeffs_of[0] = adjoint_end(adjoint, own_part, from_each_region(chunks), rates_of[0])
    grad_u = jnp.zeros((rank, own_rows), jnp.float32)
    grad_v = jnp.zeros((rank, own_rows), jnp.float32)
    for moment in reversed(range(STEPS)):
        grad_u = grad_u + jnp.dot(latent_of[moment].T, scaled_of[moment], preferred_element_type=jnp.float32)
        grad_v = grad_v + jnp.dot(coeffs_of[moment].T, signed_of[moment], preferred_element_type=jnp.float32)
    return (final_state, grad_u, grad_v)


def solution(mesh):
    finer = Mesh(
        mesh.devices.reshape(mesh.shape["region"], 4, 4, 2), ("region", "row_0", "row_1", "row_2")
    )
    in_specs = (
        P(None, REGION_ROW),
        P(None, REGION_ROW),
        P(None, REGION_ROW),
        P(REGION_ROW),
        P(REGION_ROW, None, None, None),
        P(REGION_ROW, None),
        P(REGION_ROW),
        P("region", ROW, None, None),
        P(None, REGION_ROW),
        P(None, REGION_ROW),
    )
    out_specs = (P(None, REGION_ROW), P(None, REGION_ROW), P(None, REGION_ROW))
    return jax.shard_map(local, mesh=finer, in_specs=in_specs, out_specs=out_specs, check_vma=False)
```

```python
import jax
import jax.numpy as jnp
from jax import lax
from jax.sharding import Mesh
from jax.sharding import PartitionSpec as P

STEPS = 4
ROW = ("row_0", "row_1", "row_2")
REGION_ROW = ("region", "row_0", "row_1", "row_2")


leak = 0.5


def from_each_region(chunks):
    width = chunks.shape[-1]
    padded = jnp.pad(chunks, ((0, 0), (0, 0), (0, -width % 128)))
    return lax.all_to_all(padded, "region", 0, 0, tiled=True)[..., :width]


def from_each_lane(slots):
    return lax.all_to_all(slots, ROW, 0, 0, tiled=True)


def from_every_lane(slots):
    chips = ROW[:-1]
    copies = jnp.broadcast_to(slots, (lax.axis_size(chips), *slots.shape))
    mine = lax.all_to_all(copies, chips, 0, 0, tiled=True)
    sibling = lax.ppermute(mine, ROW[-1], [(0, 1), (1, 0)])
    return jnp.stack([mine, sibling])


def split_pair(x):
    high = x.astype(jnp.bfloat16)
    low = (x - high.astype(jnp.float32)).astype(jnp.bfloat16)
    return jnp.concatenate([high, low], axis=-1)


def joined_pair(x):
    half = x.shape[-1] // 2
    return x[..., :half].astype(jnp.float32) + x[..., half:].astype(jnp.float32)


def local(
    state0,
    drive,
    cotangent,
    excitatory,
    tile_vals,
    tile_cols,
    tile_count,
    boundary_rows,
    u_factor,
    v_factor,
):
    lanes = lax.axis_size(ROW)
    groups = lax.axis_size("region")
    batch_rows, own_rows = state0.shape
    rank = v_factor.shape[0]
    own_tiles = own_rows // 128
    row_tiles = tile_vals.shape[0]
    chosen = boundary_rows.reshape(-1)
    bound_cols = chosen.shape[0]
    per_lane = own_tiles + bound_cols // 128
    tile_rows = per_lane * batch_rows
    sent = bound_cols // groups
    region_width = sent + rank
    flat_cols = tile_cols.reshape(-1)
    lane_of = flat_cols // per_lane
    cores = lax.axis_size(ROW[-1])
    side_of = (lane_of % cores != lax.axis_index(ROW[-1])).astype(jnp.int32)
    chip_of = lane_of // cores
    at_lane = flat_cols % per_lane
    live_grid = jnp.arange(tile_cols.shape[1], dtype=jnp.int32)[None, :] < tile_count[:, None]
    live_tiles = live_grid.reshape(-1)
    picks = (flat_cols[None, :] == jnp.arange(lanes * per_lane, dtype=jnp.int32)[:, None]) & live_tiles[None, :]
    picks = picks.astype(jnp.float32).reshape(lanes, per_lane, -1)
    half_rows = 16
    halves = batch_rows // half_rows
    payload_rows = tile_rows + batch_rows * 2 * rank // 128
    block_of = at_lane[:, None] * halves + jnp.arange(halves, dtype=jnp.int32)[None, :]
    picks_fwd = (
        (jnp.arange(cores, dtype=jnp.int32)[None, None, :, None, None] == side_of[:, None, None, None, None])
        & (jnp.arange(lanes // cores, dtype=jnp.int32)[None, None, None, :, None] == chip_of[:, None, None, None, None])
        & (jnp.arange(payload_rows // half_rows, dtype=jnp.int32)[None, None, None, None, :] == block_of[:, :, None, None, None])
        & live_tiles[:, None, None, None, None]
    ).astype(jnp.bfloat16)
    polarity = (2 * excitatory - 1).astype(jnp.float32)
    drive_f = drive.astype(jnp.float32)

    def forward_start(state):
        rates = jnp.tanh(state)
        signed = (polarity * rates).astype(jnp.bfloat16)
        outgoing = jnp.take(signed, chosen, axis=1).reshape(batch_rows, groups, sent)
        part_latent = jnp.dot(signed, v_factor.T, preferred_element_type=jnp.float32)
        chunks = jnp.concatenate(
            [
                jnp.moveaxis(outgoing, 1, 0).astype(jnp.float32),
                jnp.broadcast_to(part_latent, (groups, batch_rows, rank)),
            ],
            axis=2,
        )
        return rates, signed, chunks

    def forward_middle(signed, got):
        incoming = jnp.moveaxis(got[:, :, :sent], 0, 1).reshape(batch_rows, -1).astype(jnp.bfloat16)
        lane_latent = jnp.sum(got[:, :, sent:], axis=0)
        slots = jnp.concatenate(
            [
                jnp.moveaxis(signed.reshape(batch_rows, own_tiles, 128), 1, 0).reshape(-1, 128),
                incoming.reshape(batch_rows, -1),
                split_pair(lane_latent).reshape(-1, 128),
            ],
            axis=0,
        )
        return slots

    def forward_end(state, gathered):
        pair_rows = gathered[:, :, tile_rows:].reshape(lanes, batch_rows, 2 * rank)
        latent = jnp.sum(joined_pair(pair_rows), axis=0)
        stacked = gathered.reshape(*gathered.shape[:2], -1, half_rows, 128)
        blocks = jnp.einsum("shpcm,pcmrk->shrk", picks_fwd, stacked, preferred_element_type=jnp.bfloat16)
        blocks = blocks.reshape(row_tiles, -1, batch_rows, 128)
        synaptic = jnp.einsum("qjbk,qjik->bqi", blocks, tile_vals, preferred_element_type=jnp.float32)
        synaptic = synaptic.reshape(batch_rows, own_rows)
        latent_b = latent.astype(jnp.bfloat16)
        lowrank = jnp.dot(latent_b, u_factor, preferred_element_type=jnp.float32)
        return state + leak * (-state + synaptic + lowrank + drive_f), latent_b

    def adjoint_start(adjoint):
        scaled_b = (leak * adjoint).astype(jnp.bfloat16)
        part_coeff = jnp.dot(scaled_b, u_factor.T, preferred_element_type=jnp.float32)
        spread = jnp.einsum(
            "bri,rjik->brjk",
            scaled_b.reshape(batch_rows, row_tiles, 128),
            tile_vals,
            preferred_element_type=jnp.float32,
        )
        columns = jnp.einsum(
            "lts,bsk->ltbk", picks, spread.reshape(batch_rows, -1, 128), precision=lax.Precision.HIGHEST
        )
        pair_rows = split_pair(part_coeff).reshape(-1, 128)
        coeff_rows = jnp.broadcast_to(pair_rows, (lanes, *pair_rows.shape))
        tiles_rows = columns.astype(jnp.bfloat16).reshape(lanes, tile_rows, 128)
        return scaled_b, jnp.concatenate([tiles_rows, coeff_rows], axis=1)

    def adjoint_middle(got):
        everything = jnp.sum(got.astype(jnp.float32), axis=0)
        summed = everything[:tile_rows].reshape(per_lane, batch_rows, 128)
        pair_sums = everything[tile_rows:].reshape(batch_rows, 2 * rank)
        group_coeff = pair_sums[:, :rank] + pair_sums[:, rank:]
        own_part = jnp.moveaxis(summed[:own_tiles], 0, 1).reshape(batch_rows, own_rows)
        border = summed[own_tiles:].reshape(batch_rows, groups, sent)
        chunks = jnp.concatenate(
            [jnp.moveaxis(border, 1, 0), jnp.broadcast_to(group_coeff, (groups, batch_rows, rank))], axis=2
        )
        return own_part, chunks

    def adjoint_end(adjoint, own_part, back, rates):
        returned = jnp.moveaxis(back[:, :, :sent], 0, 1).reshape(batch_rows, -1)
        coeffs_b = jnp.sum(back[:, :, sent:], axis=0).astype(jnp.bfloat16)
        through = own_part.at[:, chosen].add(returned)
        total_signed = through + jnp.dot(coeffs_b, v_factor, preferred_element_type=jnp.float32)
        adjoint = (1.0 - leak) * adjoint + (1.0 - rates * rates) * polarity * total_signed
        return adjoint, coeffs_b

    def both_regions(first, second):
        got = from_each_region(jnp.concatenate([first, second], axis=2))
        return got[:, :, :region_width], got[:, :, region_width:]

    rates_of, signed_of, latent_of, scaled_of, coeffs_of = {}, {}, {}, {}, {}
    state = state0
    rates_of[0], signed_of[0], chunks = forward_start(state)
    got = from_each_region(chunks)
    scaled_of[3], lane_parts = adjoint_start(cotangent)
    got_last = from_each_lane(lane_parts)
    gathered = from_every_lane(forward_middle(signed_of[0], got))
    state, latent_of[0] = forward_end(state, gathered)
    own_last, chunks_last = adjoint_middle(got_last)
    rates_of[1], signed_of[1], chunks = forward_start(state)
    got, back_last = both_regions(chunks, chunks_last)
    gathered = from_every_lane(forward_middle(signed_of[1], got))
    state, latent_of[1] = forward_end(state, gathered)
    rates_of[2], signed_of[2], chunks = forward_start(state)
    got = from_each_region(chunks)
    gathered = from_every_lane(forward_middle(signed_of[2], got))
    state, latent_of[2] = forward_end(state, gathered)
    rates_of[3], signed_of[3], chunks_f3 = forward_start(state)
    adjoint, coeffs_of[3] = adjoint_end(cotangent, own_last, back_last, rates_of[3])
    scaled_of[2], lane_parts = adjoint_start(adjoint)
    own_part, chunks = adjoint_middle(from_each_lane(lane_parts))
    got_f3, back = both_regions(chunks_f3, chunks)
    adjoint, coeffs_of[2] = adjoint_end(adjoint, own_part, back, rates_of[2])
    scaled_of[1], lane_parts = adjoint_start(adjoint)
    gathered_f3 = from_every_lane(forward_middle(signed_of[3], got_f3))
    got = from_each_lane(lane_parts)
    final_state, latent_of[3] = forward_end(state, gathered_f3)
    own_part, chunks = adjoint_middle(got)
    adjoint, coeffs_of[1] = adjoint_end(adjoint, own_part, from_each_region(chunks), rates_of[1])
    scaled_of[0], lane_parts = adjoint_start(adjoint)
    own_part, chunks = adjoint_middle(from_each_lane(lane_parts))
    adjoint, coeffs_of[0] = adjoint_end(adjoint, own_part, from_each_region(chunks), rates_of[0])
    grad_u = jnp.zeros((rank, own_rows), jnp.float32)
    grad_v = jnp.zeros((rank, own_rows), jnp.float32)
    for moment in reversed(range(STEPS)):
        grad_u = grad_u + jnp.dot(latent_of[moment].T, scaled_of[moment], preferred_element_type=jnp.float32)
        grad_v = grad_v + jnp.dot(coeffs_of[moment].T, signed_of[moment], preferred_element_type=jnp.float32)
    return (final_state, grad_u, grad_v)


def solution(mesh):
    finer = Mesh(
        mesh.devices.reshape(mesh.shape["region"], 4, 4, 2), ("region", "row_0", "row_1", "row_2")
    )
    in_specs = (
        P(None, REGION_ROW),
        P(None, REGION_ROW),
        P(None, REGION_ROW),
        P(REGION_ROW),
        P(REGION_ROW, None, None, None),
        P(REGION_ROW, None),
        P(REGION_ROW),
        P("region", ROW, None, None),
        P(None, REGION_ROW),
        P(None, REGION_ROW),
    )
    out_specs = (P(None, REGION_ROW), P(None, REGION_ROW), P(None, REGION_ROW))
    return jax.shard_map(local, mesh=finer, in_specs=in_specs, out_specs=out_specs, check_vma=False)
```

```python
import jax
import jax.numpy as jnp
from jax import lax
from jax.sharding import Mesh
from jax.sharding import PartitionSpec as P

STEPS = 4
ROW = ("row_0", "row_1", "row_2")
REGION_ROW = ("region", "row_0", "row_1", "row_2")


leak = 0.5


def from_each_region(chunks):
    width = chunks.shape[-1]
    padded = jnp.pad(chunks, ((0, 0), (0, 0), (0, -width % 128)))
    return lax.all_to_all(padded, "region", 0, 0, tiled=True)[..., :width]


def from_each_lane(slots):
    return lax.all_to_all(slots, ROW, 0, 0, tiled=True)


def from_every_lane(slots):
    chips = ROW[:-1]
    copies = jnp.broadcast_to(slots, (lax.axis_size(chips), *slots.shape))
    mine = lax.all_to_all(copies, chips, 0, 0, tiled=True)
    sibling = lax.ppermute(mine, ROW[-1], [(0, 1), (1, 0)])
    return jnp.stack([mine, sibling])


def split_pair(x):
    high = x.astype(jnp.bfloat16)
    low = (x - high.astype(jnp.float32)).astype(jnp.bfloat16)
    return jnp.concatenate([high, low], axis=-1)


def joined_pair(x):
    half = x.shape[-1] // 2
    return x[..., :half].astype(jnp.float32) + x[..., half:].astype(jnp.float32)


def local(
    state0,
    drive,
    cotangent,
    excitatory,
    tile_vals,
    tile_cols,
    tile_count,
    boundary_rows,
    u_factor,
    v_factor,
):
    lanes = lax.axis_size(ROW)
    groups = lax.axis_size("region")
    batch_rows, own_rows = state0.shape
    rank = v_factor.shape[0]
    own_tiles = own_rows // 128
    row_tiles = tile_vals.shape[0]
    chosen = boundary_rows.reshape(-1)
    bound_cols = chosen.shape[0]
    per_lane = own_tiles + bound_cols // 128
    tile_rows = per_lane * batch_rows
    sent = bound_cols // groups
    region_width = sent + rank
    flat_cols = tile_cols.reshape(-1)
    lane_of = flat_cols // per_lane
    cores = lax.axis_size(ROW[-1])
    side_of = (lane_of % cores != lax.axis_index(ROW[-1])).astype(jnp.int32)
    chip_of = lane_of // cores
    at_lane = flat_cols % per_lane
    live_grid = jnp.arange(tile_cols.shape[1], dtype=jnp.int32)[None, :] < tile_count[:, None]
    live_tiles = live_grid.reshape(-1)
    picks = (flat_cols[None, :] == jnp.arange(lanes * per_lane, dtype=jnp.int32)[:, None]) & live_tiles[None, :]
    picks = picks.astype(jnp.float32).reshape(lanes, per_lane, -1)
    half_rows = 16
    halves = batch_rows // half_rows
    payload_rows = tile_rows + batch_rows * 2 * rank // 128
    block_of = at_lane[:, None] * halves + jnp.arange(halves, dtype=jnp.int32)[None, :]
    picks_fwd = (
        (jnp.arange(cores, dtype=jnp.int32)[None, None, :, None, None] == side_of[:, None, None, None, None])
        & (jnp.arange(lanes // cores, dtype=jnp.int32)[None, None, None, :, None] == chip_of[:, None, None, None, None])
        & (jnp.arange(payload_rows // half_rows, dtype=jnp.int32)[None, None, None, None, :] == block_of[:, :, None, None, None])
        & live_tiles[:, None, None, None, None]
    ).astype(jnp.bfloat16)
    border_to_row = (chosen[:, None] == jnp.arange(own_rows, dtype=jnp.int32)[None, :]).astype(jnp.float32)
    row_to_border = border_to_row.T.astype(jnp.bfloat16).reshape(own_rows, groups, sent)
    polarity = (2 * excitatory - 1).astype(jnp.float32)
    drive_f = drive.astype(jnp.float32)

    def forward_start(state):
        rates = jnp.tanh(state)
        signed = (polarity * rates).astype(jnp.bfloat16)
        outgoing = jnp.einsum("bn,ndk->dbk", signed, row_to_border, preferred_element_type=jnp.float32)
        part_latent = jnp.dot(signed, v_factor.T, preferred_element_type=jnp.float32)
        chunks = jnp.concatenate(
            [
                outgoing,
                jnp.broadcast_to(part_latent, (groups, batch_rows, rank)),
            ],
            axis=2,
        )
        return rates, signed, chunks

    def forward_middle(signed, got):
        incoming = jnp.moveaxis(got[:, :, :sent], 0, 1).reshape(batch_rows, -1).astype(jnp.bfloat16)
        lane_latent = jnp.sum(got[:, :, sent:], axis=0)
        slots = jnp.concatenate(
            [
                jnp.moveaxis(signed.reshape(batch_rows, own_tiles, 128), 1, 0).reshape(-1, 128),
                incoming.reshape(batch_rows, -1),
                split_pair(lane_latent).reshape(-1, 128),
            ],
            axis=0,
        )
        return slots

    def forward_end(state, gathered):
        pair_rows = gathered[:, :, tile_rows:].reshape(lanes, batch_rows, 2 * rank)
        latent = jnp.sum(joined_pair(pair_rows), axis=0)
        stacked = gathered.reshape(*gathered.shape[:2], -1, half_rows, 128)
        blocks = jnp.einsum("shpcm,pcmrk->shrk", picks_fwd, stacked, preferred_element_type=jnp.bfloat16)
        blocks = blocks.reshape(row_tiles, -1, batch_rows, 128)
        synaptic = jnp.einsum("qjbk,qjik->bqi", blocks, tile_vals, preferred_element_type=jnp.float32)
        synaptic = synaptic.reshape(batch_rows, own_rows)
        latent_b = latent.astype(jnp.bfloat16)
        lowrank = jnp.dot(latent_b, u_factor, preferred_element_type=jnp.float32)
        return state + leak * (-state + synaptic + lowrank + drive_f), latent_b

    def adjoint_start(adjoint):
        scaled_b = (leak * adjoint).astype(jnp.bfloat16)
        part_coeff = jnp.dot(scaled_b, u_factor.T, preferred_element_type=jnp.float32)
        spread = jnp.einsum(
            "bri,rjik->brjk",
            scaled_b.reshape(batch_rows, row_tiles, 128),
            tile_vals,
            preferred_element_type=jnp.float32,
        )
        columns = jnp.einsum(
            "lts,bsk->ltbk", picks, spread.reshape(batch_rows, -1, 128), precision=lax.Precision.HIGHEST
        )
        pair_rows = split_pair(part_coeff).reshape(-1, 128)
        coeff_rows = jnp.broadcast_to(pair_rows, (lanes, *pair_rows.shape))
        tiles_rows = columns.astype(jnp.bfloat16).reshape(lanes, tile_rows, 128)
        return scaled_b, jnp.concatenate([tiles_rows, coeff_rows], axis=1)

    def adjoint_middle(got):
        everything = jnp.sum(got.astype(jnp.float32), axis=0)
        summed = everything[:tile_rows].reshape(per_lane, batch_rows, 128)
        pair_sums = everything[tile_rows:].reshape(batch_rows, 2 * rank)
        group_coeff = pair_sums[:, :rank] + pair_sums[:, rank:]
        own_part = jnp.moveaxis(summed[:own_tiles], 0, 1).reshape(batch_rows, own_rows)
        border = summed[own_tiles:].reshape(batch_rows, groups, sent)
        chunks = jnp.concatenate(
            [jnp.moveaxis(border, 1, 0), jnp.broadcast_to(group_coeff, (groups, batch_rows, rank))], axis=2
        )
        return own_part, chunks

    def adjoint_end(adjoint, own_part, back, rates):
        returned = jnp.moveaxis(back[:, :, :sent], 0, 1).reshape(batch_rows, -1)
        coeffs_b = jnp.sum(back[:, :, sent:], axis=0).astype(jnp.bfloat16)
        through = own_part + jnp.dot(returned, border_to_row, precision=lax.Precision.HIGHEST)
        total_signed = through + jnp.dot(coeffs_b, v_factor, preferred_element_type=jnp.float32)
        adjoint = (1.0 - leak) * adjoint + (1.0 - rates * rates) * polarity * total_signed
        return adjoint, coeffs_b

    def both_regions(first, second):
        got = from_each_region(jnp.concatenate([first, second], axis=2))
        return got[:, :, :region_width], got[:, :, region_width:]

    rates_of, signed_of, latent_of, scaled_of, coeffs_of = {}, {}, {}, {}, {}
    state = state0
    rates_of[0], signed_of[0], chunks = forward_start(state)
    got = from_each_region(chunks)
    scaled_of[3], lane_parts = adjoint_start(cotangent)
    got_last = from_each_lane(lane_parts)
    gathered = from_every_lane(forward_middle(signed_of[0], got))
    state, latent_of[0] = forward_end(state, gathered)
    own_last, chunks_last = adjoint_middle(got_last)
    rates_of[1], signed_of[1], chunks = forward_start(state)
    got, back_last = both_regions(chunks, chunks_last)
    gathered = from_every_lane(forward_middle(signed_of[1], got))
    state, latent_of[1] = forward_end(state, gathered)
    rates_of[2], signed_of[2], chunks = forward_start(state)
    got = from_each_region(chunks)
    gathered = from_every_lane(forward_middle(signed_of[2], got))
    state, latent_of[2] = forward_end(state, gathered)
    rates_of[3], signed_of[3], chunks_f3 = forward_start(state)
    adjoint, coeffs_of[3] = adjoint_end(cotangent, own_last, back_last, rates_of[3])
    scaled_of[2], lane_parts = adjoint_start(adjoint)
    own_part, chunks = adjoint_middle(from_each_lane(lane_parts))
    got_f3, back = both_regions(chunks_f3, chunks)
    adjoint, coeffs_of[2] = adjoint_end(adjoint, own_part, back, rates_of[2])
    scaled_of[1], lane_parts = adjoint_start(adjoint)
    gathered_f3 = from_every_lane(forward_middle(signed_of[3], got_f3))
    got = from_each_lane(lane_parts)
    final_state, latent_of[3] = forward_end(state, gathered_f3)
    own_part, chunks = adjoint_middle(got)
    adjoint, coeffs_of[1] = adjoint_end(adjoint, own_part, from_each_region(chunks), rates_of[1])
    scaled_of[0], lane_parts = adjoint_start(adjoint)
    own_part, chunks = adjoint_middle(from_each_lane(lane_parts))
    adjoint, coeffs_of[0] = adjoint_end(adjoint, own_part, from_each_region(chunks), rates_of[0])
    grad_u = jnp.zeros((rank, own_rows), jnp.float32)
    grad_v = jnp.zeros((rank, own_rows), jnp.float32)
    for moment in reversed(range(STEPS)):
        grad_u = grad_u + jnp.dot(latent_of[moment].T, scaled_of[moment], preferred_element_type=jnp.float32)
        grad_v = grad_v + jnp.dot(coeffs_of[moment].T, signed_of[moment], preferred_element_type=jnp.float32)
    return (final_state, grad_u, grad_v)


def solution(mesh):
    finer = Mesh(
        mesh.devices.reshape(mesh.shape["region"], 4, 4, 2), ("region", "row_0", "row_1", "row_2")
    )
    in_specs = (
        P(None, REGION_ROW),
        P(None, REGION_ROW),
        P(None, REGION_ROW),
        P(REGION_ROW),
        P(REGION_ROW, None, None, None),
        P(REGION_ROW, None),
        P(REGION_ROW),
        P("region", ROW, None, None),
        P(None, REGION_ROW),
        P(None, REGION_ROW),
    )
    out_specs = (P(None, REGION_ROW), P(None, REGION_ROW), P(None, REGION_ROW))
    return jax.shard_map(local, mesh=finer, in_specs=in_specs, out_specs=out_specs, check_vma=False)
```

```python
import jax
import jax.numpy as jnp
from jax import lax
from jax.sharding import Mesh
from jax.sharding import PartitionSpec as P

STEPS = 4
ROW = ("row_0", "row_1", "row_2")
REGION_ROW = ("region", "row_0", "row_1", "row_2")


leak = 0.5


def from_each_region(chunks):
    width = chunks.shape[-1]
    padded = jnp.pad(chunks, ((0, 0), (0, 0), (0, -width % 128)))
    return lax.all_to_all(padded, "region", 0, 0, tiled=True)[..., :width]


def from_each_lane(slots):
    return lax.all_to_all(slots, ROW, 0, 0, tiled=True)


def from_every_lane(slots):
    chips = ROW[:-1]
    copies = jnp.broadcast_to(slots, (lax.axis_size(chips), *slots.shape))
    mine = lax.all_to_all(copies, chips, 0, 0, tiled=True)
    sibling = lax.ppermute(mine, ROW[-1], [(0, 1), (1, 0)])
    return jnp.stack([mine, sibling])


def split_pair(x):
    high = x.astype(jnp.bfloat16)
    low = (x - high.astype(jnp.float32)).astype(jnp.bfloat16)
    return jnp.concatenate([high, low], axis=-1)


def joined_pair(x):
    half = x.shape[-1] // 2
    return x[..., :half].astype(jnp.float32) + x[..., half:].astype(jnp.float32)


def local(
    state0,
    drive,
    cotangent,
    excitatory,
    tile_vals,
    tile_cols,
    tile_count,
    boundary_rows,
    u_factor,
    v_factor,
):
    lanes = lax.axis_size(ROW)
    groups = lax.axis_size("region")
    batch_rows, own_rows = state0.shape
    rank = v_factor.shape[0]
    own_tiles = own_rows // 128
    row_tiles = tile_vals.shape[0]
    chosen = boundary_rows.reshape(-1)
    bound_cols = chosen.shape[0]
    per_lane = own_tiles + bound_cols // 128
    tile_rows = per_lane * batch_rows
    sent = bound_cols // groups
    region_width = sent + rank
    flat_cols = tile_cols.reshape(-1)
    lane_of = flat_cols // per_lane
    cores = lax.axis_size(ROW[-1])
    side_of = (lane_of % cores != lax.axis_index(ROW[-1])).astype(jnp.int32)
    chip_of = lane_of // cores
    at_lane = flat_cols % per_lane
    live_grid = jnp.arange(tile_cols.shape[1], dtype=jnp.int32)[None, :] < tile_count[:, None]
    live_tiles = live_grid.reshape(-1)
    picks = (flat_cols[None, :] == jnp.arange(lanes * per_lane, dtype=jnp.int32)[:, None]) & live_tiles[None, :]
    picks = picks.astype(jnp.float32).reshape(lanes, per_lane, -1)
    half_rows = 16
    halves = batch_rows // half_rows
    block_of = at_lane[:, None] * halves + jnp.arange(halves, dtype=jnp.int32)[None, :]
    border_to_row = (chosen[:, None] == jnp.arange(own_rows, dtype=jnp.int32)[None, :]).astype(jnp.float32)
    row_to_border = border_to_row.T.astype(jnp.bfloat16).reshape(own_rows, groups, sent)
    polarity = (2 * excitatory - 1).astype(jnp.float32)
    drive_f = drive.astype(jnp.float32)

    def forward_start(state):
        rates = jnp.tanh(state)
        signed = (polarity * rates).astype(jnp.bfloat16)
        outgoing = jnp.einsum("bn,ndk->dbk", signed, row_to_border, preferred_element_type=jnp.float32)
        part_latent = jnp.dot(signed, v_factor.T, preferred_element_type=jnp.float32)
        chunks = jnp.concatenate(
            [
                outgoing,
                jnp.broadcast_to(part_latent, (groups, batch_rows, rank)),
            ],
            axis=2,
        )
        return rates, signed, chunks

    def forward_middle(signed, got):
        incoming = jnp.moveaxis(got[:, :, :sent], 0, 1).reshape(batch_rows, -1).astype(jnp.bfloat16)
        lane_latent = jnp.sum(got[:, :, sent:], axis=0)
        slots = jnp.concatenate(
            [
                jnp.moveaxis(signed.reshape(batch_rows, own_tiles, 128), 1, 0).reshape(-1, 128),
                incoming.reshape(batch_rows, -1),
                split_pair(lane_latent).reshape(-1, 128),
            ],
            axis=0,
        )
        return slots

    def forward_end(state, gathered):
        pair_rows = gathered[:, :, tile_rows:].reshape(lanes, batch_rows, 2 * rank)
        latent = jnp.sum(joined_pair(pair_rows), axis=0)
        stacked = gathered.reshape(*gathered.shape[:2], -1, half_rows, 128)
        blocks = stacked[side_of[:, None], chip_of[:, None], block_of]
        blocks = jnp.where(live_tiles[:, None, None, None], blocks, jnp.zeros((), blocks.dtype))
        blocks = blocks.reshape(row_tiles, -1, batch_rows, 128)
        synaptic = jnp.einsum("qjbk,qjik->bqi", blocks, tile_vals, preferred_element_type=jnp.float32)
        synaptic = synaptic.reshape(batch_rows, own_rows)
        latent_b = latent.astype(jnp.bfloat16)
        lowrank = jnp.dot(latent_b, u_factor, preferred_element_type=jnp.float32)
        return state + leak * (-state + synaptic + lowrank + drive_f), latent_b

    def adjoint_start(adjoint):
        scaled_b = (leak * adjoint).astype(jnp.bfloat16)
        part_coeff = jnp.dot(scaled_b, u_factor.T, preferred_element_type=jnp.float32)
        spread = jnp.einsum(
            "bri,rjik->brjk",
            scaled_b.reshape(batch_rows, row_tiles, 128),
            tile_vals,
            preferred_element_type=jnp.float32,
        )
        columns = jnp.einsum(
            "lts,bsk->ltbk", picks, spread.reshape(batch_rows, -1, 128), precision=lax.Precision.HIGHEST
        )
        pair_rows = split_pair(part_coeff).reshape(-1, 128)
        coeff_rows = jnp.broadcast_to(pair_rows, (lanes, *pair_rows.shape))
        tiles_rows = columns.astype(jnp.bfloat16).reshape(lanes, tile_rows, 128)
        return scaled_b, jnp.concatenate([tiles_rows, coeff_rows], axis=1)

    def adjoint_middle(got):
        everything = jnp.sum(got.astype(jnp.float32), axis=0)
        summed = everything[:tile_rows].reshape(per_lane, batch_rows, 128)
        pair_sums = everything[tile_rows:].reshape(batch_rows, 2 * rank)
        group_coeff = pair_sums[:, :rank] + pair_sums[:, rank:]
        own_part = jnp.moveaxis(summed[:own_tiles], 0, 1).reshape(batch_rows, own_rows)
        border = summed[own_tiles:].reshape(batch_rows, groups, sent)
        chunks = jnp.concatenate(
            [jnp.moveaxis(border, 1, 0), jnp.broadcast_to(group_coeff, (groups, batch_rows, rank))], axis=2
        )
        return own_part, chunks

    def adjoint_end(adjoint, own_part, back, rates):
        returned = jnp.moveaxis(back[:, :, :sent], 0, 1).reshape(batch_rows, -1)
        coeffs_b = jnp.sum(back[:, :, sent:], axis=0).astype(jnp.bfloat16)
        through = own_part + jnp.dot(returned, border_to_row, precision=lax.Precision.HIGHEST)
        total_signed = through + jnp.dot(coeffs_b, v_factor, preferred_element_type=jnp.float32)
        adjoint = (1.0 - leak) * adjoint + (1.0 - rates * rates) * polarity * total_signed
        return adjoint, coeffs_b

    def both_regions(first, second):
        got = from_each_region(jnp.concatenate([first, second], axis=2))
        return got[:, :, :region_width], got[:, :, region_width:]

    rates_of, signed_of, latent_of, scaled_of, coeffs_of = {}, {}, {}, {}, {}
    state = state0
    rates_of[0], signed_of[0], chunks = forward_start(state)
    got = from_each_region(chunks)
    scaled_of[3], lane_parts = adjoint_start(cotangent)
    got_last = from_each_lane(lane_parts)
    gathered = from_every_lane(forward_middle(signed_of[0], got))
    state, latent_of[0] = forward_end(state, gathered)
    own_last, chunks_last = adjoint_middle(got_last)
    rates_of[1], signed_of[1], chunks = forward_start(state)
    got, back_last = both_regions(chunks, chunks_last)
    gathered = from_every_lane(forward_middle(signed_of[1], got))
    state, latent_of[1] = forward_end(state, gathered)
    rates_of[2], signed_of[2], chunks = forward_start(state)
    got = from_each_region(chunks)
    gathered = from_every_lane(forward_middle(signed_of[2], got))
    state, latent_of[2] = forward_end(state, gathered)
    rates_of[3], signed_of[3], chunks_f3 = forward_start(state)
    adjoint, coeffs_of[3] = adjoint_end(cotangent, own_last, back_last, rates_of[3])
    scaled_of[2], lane_parts = adjoint_start(adjoint)
    own_part, chunks = adjoint_middle(from_each_lane(lane_parts))
    got_f3, back = both_regions(chunks_f3, chunks)
    adjoint, coeffs_of[2] = adjoint_end(adjoint, own_part, back, rates_of[2])
    scaled_of[1], lane_parts = adjoint_start(adjoint)
    gathered_f3 = from_every_lane(forward_middle(signed_of[3], got_f3))
    got = from_each_lane(lane_parts)
    final_state, latent_of[3] = forward_end(state, gathered_f3)
    own_part, chunks = adjoint_middle(got)
    adjoint, coeffs_of[1] = adjoint_end(adjoint, own_part, from_each_region(chunks), rates_of[1])
    scaled_of[0], lane_parts = adjoint_start(adjoint)
    own_part, chunks = adjoint_middle(from_each_lane(lane_parts))
    adjoint, coeffs_of[0] = adjoint_end(adjoint, own_part, from_each_region(chunks), rates_of[0])
    grad_u = jnp.zeros((rank, own_rows), jnp.float32)
    grad_v = jnp.zeros((rank, own_rows), jnp.float32)
    for moment in reversed(range(STEPS)):
        grad_u = grad_u + jnp.dot(latent_of[moment].T, scaled_of[moment], preferred_element_type=jnp.float32)
        grad_v = grad_v + jnp.dot(coeffs_of[moment].T, signed_of[moment], preferred_element_type=jnp.float32)
    return (final_state, grad_u, grad_v)


def solution(mesh):
    finer = Mesh(
        mesh.devices.reshape(mesh.shape["region"], 4, 4, 2), ("region", "row_0", "row_1", "row_2")
    )
    in_specs = (
        P(None, REGION_ROW),
        P(None, REGION_ROW),
        P(None, REGION_ROW),
        P(REGION_ROW),
        P(REGION_ROW, None, None, None),
        P(REGION_ROW, None),
        P(REGION_ROW),
        P("region", ROW, None, None),
        P(None, REGION_ROW),
        P(None, REGION_ROW),
    )
    out_specs = (P(None, REGION_ROW), P(None, REGION_ROW), P(None, REGION_ROW))
    return jax.shard_map(local, mesh=finer, in_specs=in_specs, out_specs=out_specs, check_vma=False)
```

```python
import jax
import jax.numpy as jnp
from jax import lax
from jax.sharding import Mesh
from jax.sharding import PartitionSpec as P

STEPS = 4
ROW = ("row_0", "row_1", "row_2")
REGION_ROW = ("region", "row_0", "row_1", "row_2")


leak = 0.5


def from_each_region(chunks):
    width = chunks.shape[-1]
    padded = jnp.pad(chunks, ((0, 0), (0, 0), (0, -width % 128)))
    return lax.all_to_all(padded, "region", 0, 0, tiled=True)[..., :width]


def from_each_lane(slots):
    return lax.all_to_all(slots, ROW, 0, 0, tiled=True)


def from_every_lane(slots):
    chips = ROW[:-1]
    copies = jnp.broadcast_to(slots, (lax.axis_size(chips), *slots.shape))
    mine = lax.all_to_all(copies, chips, 0, 0, tiled=True)
    sibling = lax.ppermute(mine, ROW[-1], [(0, 1), (1, 0)])
    return jnp.stack([mine, sibling])


def split_pair(x):
    high = x.astype(jnp.bfloat16)
    low = (x - high.astype(jnp.float32)).astype(jnp.bfloat16)
    return jnp.concatenate([high, low], axis=-1)


def joined_pair(x):
    half = x.shape[-1] // 2
    return x[..., :half].astype(jnp.float32) + x[..., half:].astype(jnp.float32)


def local(
    state0,
    drive,
    cotangent,
    excitatory,
    tile_vals,
    tile_cols,
    tile_count,
    boundary_rows,
    u_factor,
    v_factor,
):
    lanes = lax.axis_size(ROW)
    groups = lax.axis_size("region")
    batch_rows, own_rows = state0.shape
    rank = v_factor.shape[0]
    own_tiles = own_rows // 128
    row_tiles = tile_vals.shape[0]
    chosen = boundary_rows.reshape(-1)
    bound_cols = chosen.shape[0]
    per_lane = own_tiles + bound_cols // 128
    tile_rows = per_lane * batch_rows
    sent = bound_cols // groups
    region_width = sent + rank
    flat_cols = tile_cols.reshape(-1)
    lane_of = flat_cols // per_lane
    cores = lax.axis_size(ROW[-1])
    side_of = (lane_of % cores != lax.axis_index(ROW[-1])).astype(jnp.int32)
    chip_of = lane_of // cores
    at_lane = flat_cols % per_lane
    live_grid = jnp.arange(tile_cols.shape[1], dtype=jnp.int32)[None, :] < tile_count[:, None]
    live_tiles = live_grid.reshape(-1)
    picks = (flat_cols[None, :] == jnp.arange(lanes * per_lane, dtype=jnp.int32)[:, None]) & live_tiles[None, :]
    picks = picks.astype(jnp.float32).reshape(lanes, per_lane, -1)
    half_rows = 16
    halves = batch_rows // half_rows
    payload_rows = tile_rows + batch_rows * 2 * rank // 128
    block_of = at_lane[:, None] * halves + jnp.arange(halves, dtype=jnp.int32)[None, :]
    picks_fwd = (
        (jnp.arange(cores, dtype=jnp.int32)[None, None, :, None, None] == side_of[:, None, None, None, None])
        & (jnp.arange(lanes // cores, dtype=jnp.int32)[None, None, None, :, None] == chip_of[:, None, None, None, None])
        & (jnp.arange(payload_rows // half_rows, dtype=jnp.int32)[None, None, None, None, :] == block_of[:, :, None, None, None])
        & live_tiles[:, None, None, None, None]
    ).astype(jnp.bfloat16)
    border_to_row = (chosen[:, None] == jnp.arange(own_rows, dtype=jnp.int32)[None, :]).astype(jnp.float32)
    row_to_border = border_to_row.T.astype(jnp.bfloat16).reshape(own_rows, groups, sent)
    polarity = (2 * excitatory - 1).astype(jnp.float32)
    drive_f = drive.astype(jnp.float32)

    def forward_start(state):
        rates = jnp.tanh(state)
        signed = (polarity * rates).astype(jnp.bfloat16)
        outgoing = jnp.einsum("bn,ndk->dbk", signed, row_to_border, preferred_element_type=jnp.float32)
        part_latent = jnp.dot(signed, v_factor.T, preferred_element_type=jnp.float32)
        chunks = jnp.concatenate(
            [
                outgoing,
                jnp.broadcast_to(part_latent, (groups, batch_rows, rank)),
            ],
            axis=2,
        )
        return rates, signed, chunks

    def forward_middle(signed, got):
        incoming = jnp.moveaxis(got[:, :, :sent], 0, 1).reshape(batch_rows, -1).astype(jnp.bfloat16)
        lane_latent = jnp.sum(got[:, :, sent:], axis=0)
        slots = jnp.concatenate(
            [
                jnp.moveaxis(signed.reshape(batch_rows, own_tiles, 128), 1, 0).reshape(-1, 128),
                incoming.reshape(batch_rows, -1),
                split_pair(lane_latent).reshape(-1, 128),
            ],
            axis=0,
        )
        return slots

    def forward_end(state, gathered):
        pair_rows = gathered[:, :, tile_rows:].reshape(lanes, batch_rows, 2 * rank)
        latent = jnp.sum(joined_pair(pair_rows), axis=0)
        stacked = gathered.reshape(*gathered.shape[:2], -1, half_rows, 128)
        blocks = jnp.einsum("shpcm,pcmrk->shrk", picks_fwd, stacked, preferred_element_type=jnp.bfloat16)
        blocks = blocks.reshape(row_tiles, -1, batch_rows, 128)
        synaptic = jnp.einsum("qjbk,qjik->bqi", blocks, tile_vals, preferred_element_type=jnp.float32)
        synaptic = synaptic.reshape(batch_rows, own_rows)
        latent_b = latent.astype(jnp.bfloat16)
        lowrank = jnp.dot(latent_b, u_factor, preferred_element_type=jnp.float32)
        return state + leak * (-state + synaptic + lowrank + drive_f), latent_b

    def adjoint_start(adjoint):
        scaled_b = (leak * adjoint).astype(jnp.bfloat16)
        part_coeff = jnp.dot(scaled_b, u_factor.T, preferred_element_type=jnp.float32)
        spread = jnp.einsum(
            "bri,rjik->brjk",
            scaled_b.reshape(batch_rows, row_tiles, 128),
            tile_vals,
            preferred_element_type=jnp.float32,
        )
        columns = jnp.einsum(
            "lts,bsk->ltbk", picks, spread.reshape(batch_rows, -1, 128), precision=lax.Precision.HIGHEST
        )
        pair_rows = split_pair(part_coeff).reshape(-1, 128)
        coeff_rows = jnp.broadcast_to(pair_rows, (lanes, *pair_rows.shape))
        tiles_rows = columns.astype(jnp.bfloat16).reshape(lanes, tile_rows, 128)
        return scaled_b, jnp.concatenate([tiles_rows, coeff_rows], axis=1)

    def adjoint_middle(got):
        everything = jnp.sum(got.astype(jnp.float32), axis=0)
        summed = everything[:tile_rows].reshape(per_lane, batch_rows, 128)
        pair_sums = everything[tile_rows:].reshape(batch_rows, 2 * rank)
        group_coeff = pair_sums[:, :rank] + pair_sums[:, rank:]
        own_part = jnp.moveaxis(summed[:own_tiles], 0, 1).reshape(batch_rows, own_rows)
        border = summed[own_tiles:].reshape(batch_rows, groups, sent)
        chunks = jnp.concatenate(
            [jnp.moveaxis(border, 1, 0), jnp.broadcast_to(group_coeff, (groups, batch_rows, rank))], axis=2
        )
        return own_part, chunks

    def adjoint_end(adjoint, own_part, back, rates):
        coeffs_b = jnp.sum(back[:, :, sent:], axis=0).astype(jnp.bfloat16)
        returned = jnp.einsum(
            "gbk,gkn->bn", back[:, :, :sent], border_to_row.reshape(groups, sent, own_rows), precision=lax.Precision.HIGHEST
        )
        through = own_part + returned
        total_signed = through + jnp.dot(coeffs_b, v_factor, preferred_element_type=jnp.float32)
        adjoint = (1.0 - leak) * adjoint + (1.0 - rates * rates) * polarity * total_signed
        return adjoint, coeffs_b

    def both_regions(first, second):
        got = from_each_region(jnp.concatenate([first, second], axis=2))
        return got[:, :, :region_width], got[:, :, region_width:]

    rates_of, signed_of, latent_of, scaled_of, coeffs_of = {}, {}, {}, {}, {}
    state = state0
    rates_of[0], signed_of[0], chunks = forward_start(state)
    got = from_each_region(chunks)
    scaled_of[3], lane_parts = adjoint_start(cotangent)
    got_last = from_each_lane(lane_parts)
    gathered = from_every_lane(forward_middle(signed_of[0], got))
    state, latent_of[0] = forward_end(state, gathered)
    own_last, chunks_last = adjoint_middle(got_last)
    rates_of[1], signed_of[1], chunks = forward_start(state)
    got, back_last = both_regions(chunks, chunks_last)
    gathered = from_every_lane(forward_middle(signed_of[1], got))
    state, latent_of[1] = forward_end(state, gathered)
    rates_of[2], signed_of[2], chunks = forward_start(state)
    got = from_each_region(chunks)
    gathered = from_every_lane(forward_middle(signed_of[2], got))
    state, latent_of[2] = forward_end(state, gathered)
    rates_of[3], signed_of[3], chunks_f3 = forward_start(state)
    adjoint, coeffs_of[3] = adjoint_end(cotangent, own_last, back_last, rates_of[3])
    scaled_of[2], lane_parts = adjoint_start(adjoint)
    own_part, chunks = adjoint_middle(from_each_lane(lane_parts))
    got_f3, back = both_regions(chunks_f3, chunks)
    adjoint, coeffs_of[2] = adjoint_end(adjoint, own_part, back, rates_of[2])
    scaled_of[1], lane_parts = adjoint_start(adjoint)
    gathered_f3 = from_every_lane(forward_middle(signed_of[3], got_f3))
    got = from_each_lane(lane_parts)
    final_state, latent_of[3] = forward_end(state, gathered_f3)
    own_part, chunks = adjoint_middle(got)
    adjoint, coeffs_of[1] = adjoint_end(adjoint, own_part, from_each_region(chunks), rates_of[1])
    scaled_of[0], lane_parts = adjoint_start(adjoint)
    own_part, chunks = adjoint_middle(from_each_lane(lane_parts))
    adjoint, coeffs_of[0] = adjoint_end(adjoint, own_part, from_each_region(chunks), rates_of[0])
    grad_u = jnp.zeros((rank, own_rows), jnp.float32)
    grad_v = jnp.zeros((rank, own_rows), jnp.float32)
    for moment in reversed(range(STEPS)):
        grad_u = grad_u + jnp.dot(latent_of[moment].T, scaled_of[moment], preferred_element_type=jnp.float32)
        grad_v = grad_v + jnp.dot(coeffs_of[moment].T, signed_of[moment], preferred_element_type=jnp.float32)
    return (final_state, grad_u, grad_v)


def solution(mesh):
    finer = Mesh(
        mesh.devices.reshape(mesh.shape["region"], 4, 4, 2), ("region", "row_0", "row_1", "row_2")
    )
    in_specs = (
        P(None, REGION_ROW),
        P(None, REGION_ROW),
        P(None, REGION_ROW),
        P(REGION_ROW),
        P(REGION_ROW, None, None, None),
        P(REGION_ROW, None),
        P(REGION_ROW),
        P("region", ROW, None, None),
        P(None, REGION_ROW),
        P(None, REGION_ROW),
    )
    out_specs = (P(None, REGION_ROW), P(None, REGION_ROW), P(None, REGION_ROW))
    return jax.shard_map(local, mesh=finer, in_specs=in_specs, out_specs=out_specs, check_vma=False)
```

```python
import jax
import jax.numpy as jnp
from jax import lax
from jax.sharding import Mesh
from jax.sharding import PartitionSpec as P

STEPS = 4
ROW = ("row_0", "row_1", "row_2")
REGION_ROW = ("region", "row_0", "row_1", "row_2")


leak = 0.5


def from_each_region(chunks):
    width = chunks.shape[-1]
    padded = jnp.pad(chunks, ((0, 0), (0, 0), (0, -width % 128)))
    return lax.all_to_all(padded, "region", 0, 0, tiled=True)[..., :width]


def from_each_lane(slots):
    return lax.all_to_all(slots, ROW, 0, 0, tiled=True)


def from_every_lane(slots):
    chips = ROW[:-1]
    copies = jnp.broadcast_to(slots, (lax.axis_size(chips), *slots.shape))
    mine = lax.all_to_all(copies, chips, 0, 0, tiled=True)
    sibling = lax.ppermute(mine, ROW[-1], [(0, 1), (1, 0)])
    return jnp.stack([mine, sibling])


def split_pair(x):
    high = x.astype(jnp.bfloat16)
    low = (x - high.astype(jnp.float32)).astype(jnp.bfloat16)
    return jnp.concatenate([high, low], axis=-1)


def joined_pair(x):
    half = x.shape[-1] // 2
    return x[..., :half].astype(jnp.float32) + x[..., half:].astype(jnp.float32)


def local(
    state0,
    drive,
    cotangent,
    excitatory,
    tile_vals,
    tile_cols,
    tile_count,
    boundary_rows,
    u_factor,
    v_factor,
):
    lanes = lax.axis_size(ROW)
    groups = lax.axis_size("region")
    batch_rows, own_rows = state0.shape
    rank = v_factor.shape[0]
    own_tiles = own_rows // 128
    row_tiles = tile_vals.shape[0]
    chosen = boundary_rows.reshape(-1)
    bound_cols = chosen.shape[0]
    per_lane = own_tiles + bound_cols // 128
    tile_rows = per_lane * batch_rows
    sent = bound_cols // groups
    region_width = sent + rank
    flat_cols = tile_cols.reshape(-1)
    lane_of = flat_cols // per_lane
    cores = lax.axis_size(ROW[-1])
    side_of = (lane_of % cores != lax.axis_index(ROW[-1])).astype(jnp.int32)
    chip_of = lane_of // cores
    at_lane = flat_cols % per_lane
    live_grid = jnp.arange(tile_cols.shape[1], dtype=jnp.int32)[None, :] < tile_count[:, None]
    live_tiles = live_grid.reshape(-1)
    picks = (flat_cols[None, :] == jnp.arange(lanes * per_lane, dtype=jnp.int32)[:, None]) & live_tiles[None, :]
    picks = picks.astype(jnp.float32).reshape(lanes, per_lane, -1)
    half_rows = 16
    halves = batch_rows // half_rows
    payload_rows = tile_rows + batch_rows * 2 * rank // 128
    block_of = at_lane[:, None] * halves + jnp.arange(halves, dtype=jnp.int32)[None, :]
    picks_fwd = (
        (jnp.arange(cores, dtype=jnp.int32)[None, None, :, None, None] == side_of[:, None, None, None, None])
        & (jnp.arange(lanes // cores, dtype=jnp.int32)[None, None, None, :, None] == chip_of[:, None, None, None, None])
        & (jnp.arange(payload_rows // half_rows, dtype=jnp.int32)[None, None, None, None, :] == block_of[:, :, None, None, None])
        & live_tiles[:, None, None, None, None]
    ).astype(jnp.bfloat16)
    border_to_row = (chosen[:, None] == jnp.arange(own_rows, dtype=jnp.int32)[None, :]).astype(jnp.float32)
    row_to_border = border_to_row.T.astype(jnp.bfloat16).reshape(own_rows, groups, sent)
    border_split = jnp.eye(bound_cols, dtype=jnp.float32).reshape(bound_cols, groups, sent)
    polarity = (2 * excitatory - 1).astype(jnp.float32)
    drive_f = drive.astype(jnp.float32)

    def forward_start(state):
        rates = jnp.tanh(state)
        signed = (polarity * rates).astype(jnp.bfloat16)
        outgoing = jnp.einsum("bn,ndk->dbk", signed, row_to_border, preferred_element_type=jnp.float32)
        part_latent = jnp.dot(signed, v_factor.T, preferred_element_type=jnp.float32)
        chunks = jnp.concatenate(
            [
                outgoing,
                jnp.broadcast_to(part_latent, (groups, batch_rows, rank)),
            ],
            axis=2,
        )
        return rates, signed, chunks

    def forward_middle(signed, got):
        incoming = jnp.moveaxis(got[:, :, :sent], 0, 1).reshape(batch_rows, -1).astype(jnp.bfloat16)
        lane_latent = jnp.sum(got[:, :, sent:], axis=0)
        slots = jnp.concatenate(
            [
                jnp.moveaxis(signed.reshape(batch_rows, own_tiles, 128), 1, 0).reshape(-1, 128),
                incoming.reshape(batch_rows, -1),
                split_pair(lane_latent).reshape(-1, 128),
            ],
            axis=0,
        )
        return slots

    def forward_end(state, gathered):
        pair_rows = gathered[:, :, tile_rows:].reshape(lanes, batch_rows, 2 * rank)
        latent = jnp.sum(joined_pair(pair_rows), axis=0)
        stacked = gathered.reshape(*gathered.shape[:2], -1, half_rows, 128)
        blocks = jnp.einsum("shpcm,pcmrk->shrk", picks_fwd, stacked, preferred_element_type=jnp.bfloat16)
        blocks = blocks.reshape(row_tiles, -1, batch_rows, 128)
        synaptic = jnp.einsum("qjbk,qjik->bqi", blocks, tile_vals, preferred_element_type=jnp.float32)
        synaptic = synaptic.reshape(batch_rows, own_rows)
        latent_b = latent.astype(jnp.bfloat16)
        lowrank = jnp.dot(latent_b, u_factor, preferred_element_type=jnp.float32)
        return state + leak * (-state + synaptic + lowrank + drive_f), latent_b

    def adjoint_start(adjoint):
        scaled_b = (leak * adjoint).astype(jnp.bfloat16)
        part_coeff = jnp.dot(scaled_b, u_factor.T, preferred_element_type=jnp.float32)
        spread = jnp.einsum(
            "bri,rjik->brjk",
            scaled_b.reshape(batch_rows, row_tiles, 128),
            tile_vals,
            preferred_element_type=jnp.float32,
        )
        columns = jnp.einsum(
            "lts,bsk->ltbk", picks, spread.reshape(batch_rows, -1, 128), precision=lax.Precision.HIGHEST
        )
        pair_rows = split_pair(part_coeff).reshape(-1, 128)
        coeff_rows = jnp.broadcast_to(pair_rows, (lanes, *pair_rows.shape))
        tiles_rows = columns.astype(jnp.bfloat16).reshape(lanes, tile_rows, 128)
        return scaled_b, jnp.concatenate([tiles_rows, coeff_rows], axis=1)

    def adjoint_middle(got):
        everything = jnp.sum(got.astype(jnp.float32), axis=0)
        summed = everything[:tile_rows].reshape(per_lane, batch_rows, 128)
        pair_sums = everything[tile_rows:].reshape(batch_rows, 2 * rank)
        group_coeff = pair_sums[:, :rank] + pair_sums[:, rank:]
        own_part = jnp.moveaxis(summed[:own_tiles], 0, 1).reshape(batch_rows, own_rows)
        border = jnp.einsum(
            "bc,cgk->gbk", summed[own_tiles], border_split, precision=lax.Precision.HIGHEST
        )
        chunks = jnp.concatenate([border, jnp.broadcast_to(group_coeff, (groups, batch_rows, rank))], axis=2)
        return own_part, chunks

    def adjoint_end(adjoint, own_part, back, rates):
        coeffs_b = jnp.sum(back[:, :, sent:], axis=0).astype(jnp.bfloat16)
        returned = jnp.einsum(
            "gbk,gkn->bn", back[:, :, :sent], border_to_row.reshape(groups, sent, own_rows), precision=lax.Precision.HIGHEST
        )
        through = own_part + returned
        total_signed = through + jnp.dot(coeffs_b, v_factor, preferred_element_type=jnp.float32)
        adjoint = (1.0 - leak) * adjoint + (1.0 - rates * rates) * polarity * total_signed
        return adjoint, coeffs_b

    def both_regions(first, second):
        got = from_each_region(jnp.concatenate([first, second], axis=2))
        return got[:, :, :region_width], got[:, :, region_width:]

    rates_of, signed_of, latent_of, scaled_of, coeffs_of = {}, {}, {}, {}, {}
    state = state0
    rates_of[0], signed_of[0], chunks = forward_start(state)
    got = from_each_region(chunks)
    scaled_of[3], lane_parts = adjoint_start(cotangent)
    got_last = from_each_lane(lane_parts)
    gathered = from_every_lane(forward_middle(signed_of[0], got))
    state, latent_of[0] = forward_end(state, gathered)
    own_last, chunks_last = adjoint_middle(got_last)
    rates_of[1], signed_of[1], chunks = forward_start(state)
    got, back_last = both_regions(chunks, chunks_last)
    gathered = from_every_lane(forward_middle(signed_of[1], got))
    state, latent_of[1] = forward_end(state, gathered)
    rates_of[2], signed_of[2], chunks = forward_start(state)
    got = from_each_region(chunks)
    gathered = from_every_lane(forward_middle(signed_of[2], got))
    state, latent_of[2] = forward_end(state, gathered)
    rates_of[3], signed_of[3], chunks_f3 = forward_start(state)
    adjoint, coeffs_of[3] = adjoint_end(cotangent, own_last, back_last, rates_of[3])
    scaled_of[2], lane_parts = adjoint_start(adjoint)
    own_part, chunks = adjoint_middle(from_each_lane(lane_parts))
    got_f3, back = both_regions(chunks_f3, chunks)
    adjoint, coeffs_of[2] = adjoint_end(adjoint, own_part, back, rates_of[2])
    scaled_of[1], lane_parts = adjoint_start(adjoint)
    gathered_f3 = from_every_lane(forward_middle(signed_of[3], got_f3))
    got = from_each_lane(lane_parts)
    final_state, latent_of[3] = forward_end(state, gathered_f3)
    own_part, chunks = adjoint_middle(got)
    adjoint, coeffs_of[1] = adjoint_end(adjoint, own_part, from_each_region(chunks), rates_of[1])
    scaled_of[0], lane_parts = adjoint_start(adjoint)
    own_part, chunks = adjoint_middle(from_each_lane(lane_parts))
    adjoint, coeffs_of[0] = adjoint_end(adjoint, own_part, from_each_region(chunks), rates_of[0])
    grad_u = jnp.zeros((rank, own_rows), jnp.float32)
    grad_v = jnp.zeros((rank, own_rows), jnp.float32)
    for moment in reversed(range(STEPS)):
        grad_u = grad_u + jnp.dot(latent_of[moment].T, scaled_of[moment], preferred_element_type=jnp.float32)
        grad_v = grad_v + jnp.dot(coeffs_of[moment].T, signed_of[moment], preferred_element_type=jnp.float32)
    return (final_state, grad_u, grad_v)


def solution(mesh):
    finer = Mesh(
        mesh.devices.reshape(mesh.shape["region"], 4, 4, 2), ("region", "row_0", "row_1", "row_2")
    )
    in_specs = (
        P(None, REGION_ROW),
        P(None, REGION_ROW),
        P(None, REGION_ROW),
        P(REGION_ROW),
        P(REGION_ROW, None, None, None),
        P(REGION_ROW, None),
        P(REGION_ROW),
        P("region", ROW, None, None),
        P(None, REGION_ROW),
        P(None, REGION_ROW),
    )
    out_specs = (P(None, REGION_ROW), P(None, REGION_ROW), P(None, REGION_ROW))
    return jax.shard_map(local, mesh=finer, in_specs=in_specs, out_specs=out_specs, check_vma=False)
```

```python
import jax
import jax.numpy as jnp
from jax import lax
from jax.sharding import Mesh
from jax.sharding import PartitionSpec as P

STEPS = 4
ROW = ("row_0", "row_1", "row_2")
REGION_ROW = ("region", "row_0", "row_1", "row_2")


leak = 0.5


def from_each_region(chunks):
    width = chunks.shape[-1]
    padded = jnp.pad(chunks, ((0, 0), (0, 0), (0, -width % 128)))
    return lax.all_to_all(padded, "region", 0, 0, tiled=True)[..., :width]


def from_each_lane(slots):
    return lax.all_to_all(slots, ROW, 0, 0, tiled=True)


def from_every_lane(slots):
    chips = ROW[:-1]
    copies = jnp.broadcast_to(slots, (lax.axis_size(chips), *slots.shape))
    mine = lax.all_to_all(copies, chips, 0, 0, tiled=True)
    sibling = lax.ppermute(mine, ROW[-1], [(0, 1), (1, 0)])
    return jnp.stack([mine, sibling])


def split_pair(x):
    high = x.astype(jnp.bfloat16)
    low = (x - high.astype(jnp.float32)).astype(jnp.bfloat16)
    return jnp.concatenate([high, low], axis=-1)


def pair_rows(x):
    flat = x.reshape(-1, 128)
    high = flat.astype(jnp.bfloat16)
    low = (flat - high.astype(jnp.float32)).astype(jnp.bfloat16)
    return jnp.concatenate([high, low], axis=0)


def joined_rows(x, shape):
    half = x.shape[-2] // 2
    return (x[..., :half, :].astype(jnp.float32) + x[..., half:, :].astype(jnp.float32)).reshape(*x.shape[:-2], *shape)


def joined_pair(x):
    half = x.shape[-1] // 2
    return x[..., :half].astype(jnp.float32) + x[..., half:].astype(jnp.float32)


def local(
    state0,
    drive,
    cotangent,
    excitatory,
    tile_vals,
    tile_cols,
    tile_count,
    boundary_rows,
    u_factor,
    v_factor,
):
    lanes = lax.axis_size(ROW)
    groups = lax.axis_size("region")
    batch_rows, own_rows = state0.shape
    rank = v_factor.shape[0]
    own_tiles = own_rows // 128
    row_tiles = tile_vals.shape[0]
    chosen = boundary_rows.reshape(-1)
    bound_cols = chosen.shape[0]
    per_lane = own_tiles + bound_cols // 128
    tile_rows = per_lane * batch_rows
    sent = bound_cols // groups
    region_width = sent + rank
    flat_cols = tile_cols.reshape(-1)
    lane_of = flat_cols // per_lane
    cores = lax.axis_size(ROW[-1])
    side_of = (lane_of % cores != lax.axis_index(ROW[-1])).astype(jnp.int32)
    chip_of = lane_of // cores
    at_lane = flat_cols % per_lane
    live_grid = jnp.arange(tile_cols.shape[1], dtype=jnp.int32)[None, :] < tile_count[:, None]
    live_tiles = live_grid.reshape(-1)
    picks = (flat_cols[None, :] == jnp.arange(lanes * per_lane, dtype=jnp.int32)[:, None]) & live_tiles[None, :]
    picks = picks.astype(jnp.float32).reshape(lanes, per_lane, -1)
    half_rows = 16
    halves = batch_rows // half_rows
    payload_rows = tile_rows + batch_rows * 2 * rank // 128
    block_of = at_lane[:, None] * halves + jnp.arange(halves, dtype=jnp.int32)[None, :]
    picks_fwd = (
        (jnp.arange(cores, dtype=jnp.int32)[None, None, :, None, None] == side_of[:, None, None, None, None])
        & (jnp.arange(lanes // cores, dtype=jnp.int32)[None, None, None, :, None] == chip_of[:, None, None, None, None])
        & (jnp.arange(payload_rows // half_rows, dtype=jnp.int32)[None, None, None, None, :] == block_of[:, :, None, None, None])
        & live_tiles[:, None, None, None, None]
    ).astype(jnp.bfloat16)
    border_to_row = (chosen[:, None] == jnp.arange(own_rows, dtype=jnp.int32)[None, :]).astype(jnp.float32)
    row_to_border = border_to_row.T.astype(jnp.bfloat16).reshape(own_rows, groups, sent)
    polarity = (2 * excitatory - 1).astype(jnp.float32)
    drive_f = drive.astype(jnp.float32)

    def forward_start(state):
        rates = jnp.tanh(state)
        signed = (polarity * rates).astype(jnp.bfloat16)
        outgoing = jnp.einsum("bn,ndk->dbk", signed, row_to_border, preferred_element_type=jnp.float32)
        part_latent = jnp.dot(signed, v_factor.T, preferred_element_type=jnp.float32)
        chunks = jnp.concatenate(
            [
                outgoing,
                jnp.broadcast_to(part_latent, (groups, batch_rows, rank)),
            ],
            axis=2,
        )
        return rates, signed, chunks

    def forward_middle(signed, got):
        incoming = jnp.moveaxis(got[:, :, :sent], 0, 1).reshape(batch_rows, -1).astype(jnp.bfloat16)
        lane_latent = jnp.sum(got[:, :, sent:], axis=0)
        slots = jnp.concatenate(
            [
                jnp.moveaxis(signed.reshape(batch_rows, own_tiles, 128), 1, 0).reshape(-1, 128),
                incoming.reshape(batch_rows, -1),
                pair_rows(lane_latent),
            ],
            axis=0,
        )
        return slots

    def forward_end(state, gathered):
        latent = jnp.sum(joined_rows(gathered[:, :, tile_rows:], (batch_rows, rank)), axis=(0, 1))
        stacked = gathered.reshape(*gathered.shape[:2], -1, half_rows, 128)
        blocks = jnp.einsum("shpcm,pcmrk->shrk", picks_fwd, stacked, preferred_element_type=jnp.bfloat16)
        blocks = blocks.reshape(row_tiles, -1, batch_rows, 128)
        synaptic = jnp.einsum("qjbk,qjik->bqi", blocks, tile_vals, preferred_element_type=jnp.float32)
        synaptic = synaptic.reshape(batch_rows, own_rows)
        latent_b = latent.astype(jnp.bfloat16)
        lowrank = jnp.dot(latent_b, u_factor, preferred_element_type=jnp.float32)
        return state + leak * (-state + synaptic + lowrank + drive_f), latent_b

    def adjoint_start(adjoint):
        scaled_b = (leak * adjoint).astype(jnp.bfloat16)
        part_coeff = jnp.dot(scaled_b, u_factor.T, preferred_element_type=jnp.float32)
        spread = jnp.einsum(
            "bri,rjik->brjk",
            scaled_b.reshape(batch_rows, row_tiles, 128),
            tile_vals,
            preferred_element_type=jnp.float32,
        )
        columns = jnp.einsum(
            "lts,bsk->ltbk", picks, spread.reshape(batch_rows, -1, 128), precision=lax.Precision.HIGHEST
        )
        coeff_pair = pair_rows(part_coeff)
        coeff_rows = jnp.broadcast_to(coeff_pair, (lanes, *coeff_pair.shape))
        tiles_rows = columns.astype(jnp.bfloat16).reshape(lanes, tile_rows, 128)
        return scaled_b, jnp.concatenate([tiles_rows, coeff_rows], axis=1)

    def adjoint_middle(got):
        everything = jnp.sum(got.astype(jnp.float32), axis=0)
        summed = everything[:tile_rows].reshape(per_lane, batch_rows, 128)
        group_coeff = joined_rows(everything[tile_rows:], (batch_rows, rank))
        own_part = jnp.moveaxis(summed[:own_tiles], 0, 1).reshape(batch_rows, own_rows)
        border = summed[own_tiles:].reshape(batch_rows, groups, sent)
        chunks = jnp.concatenate(
            [jnp.moveaxis(border, 1, 0), jnp.broadcast_to(group_coeff, (groups, batch_rows, rank))], axis=2
        )
        return own_part, chunks

    def adjoint_end(adjoint, own_part, back, rates):
        coeffs_b = jnp.sum(back[:, :, sent:], axis=0).astype(jnp.bfloat16)
        returned = jnp.einsum(
            "gbk,gkn->bn", back[:, :, :sent], border_to_row.reshape(groups, sent, own_rows), precision=lax.Precision.HIGHEST
        )
        through = own_part + returned
        total_signed = through + jnp.dot(coeffs_b, v_factor, preferred_element_type=jnp.float32)
        adjoint = (1.0 - leak) * adjoint + (1.0 - rates * rates) * polarity * total_signed
        return adjoint, coeffs_b

    def both_regions(first, second):
        got = from_each_region(jnp.concatenate([first, second], axis=2))
        return got[:, :, :region_width], got[:, :, region_width:]

    rates_of, signed_of, latent_of, scaled_of, coeffs_of = {}, {}, {}, {}, {}
    state = state0
    rates_of[0], signed_of[0], chunks = forward_start(state)
    got = from_each_region(chunks)
    scaled_of[3], lane_parts = adjoint_start(cotangent)
    got_last = from_each_lane(lane_parts)
    gathered = from_every_lane(forward_middle(signed_of[0], got))
    state, latent_of[0] = forward_end(state, gathered)
    own_last, chunks_last = adjoint_middle(got_last)
    rates_of[1], signed_of[1], chunks = forward_start(state)
    got, back_last = both_regions(chunks, chunks_last)
    gathered = from_every_lane(forward_middle(signed_of[1], got))
    state, latent_of[1] = forward_end(state, gathered)
    rates_of[2], signed_of[2], chunks = forward_start(state)
    got = from_each_region(chunks)
    gathered = from_every_lane(forward_middle(signed_of[2], got))
    state, latent_of[2] = forward_end(state, gathered)
    rates_of[3], signed_of[3], chunks_f3 = forward_start(state)
    adjoint, coeffs_of[3] = adjoint_end(cotangent, own_last, back_last, rates_of[3])
    scaled_of[2], lane_parts = adjoint_start(adjoint)
    own_part, chunks = adjoint_middle(from_each_lane(lane_parts))
    got_f3, back = both_regions(chunks_f3, chunks)
    adjoint, coeffs_of[2] = adjoint_end(adjoint, own_part, back, rates_of[2])
    scaled_of[1], lane_parts = adjoint_start(adjoint)
    gathered_f3 = from_every_lane(forward_middle(signed_of[3], got_f3))
    got = from_each_lane(lane_parts)
    final_state, latent_of[3] = forward_end(state, gathered_f3)
    own_part, chunks = adjoint_middle(got)
    adjoint, coeffs_of[1] = adjoint_end(adjoint, own_part, from_each_region(chunks), rates_of[1])
    scaled_of[0], lane_parts = adjoint_start(adjoint)
    own_part, chunks = adjoint_middle(from_each_lane(lane_parts))
    adjoint, coeffs_of[0] = adjoint_end(adjoint, own_part, from_each_region(chunks), rates_of[0])
    grad_u = jnp.zeros((rank, own_rows), jnp.float32)
    grad_v = jnp.zeros((rank, own_rows), jnp.float32)
    for moment in reversed(range(STEPS)):
        grad_u = grad_u + jnp.dot(latent_of[moment].T, scaled_of[moment], preferred_element_type=jnp.float32)
        grad_v = grad_v + jnp.dot(coeffs_of[moment].T, signed_of[moment], preferred_element_type=jnp.float32)
    return (final_state, grad_u, grad_v)


def solution(mesh):
    finer = Mesh(
        mesh.devices.reshape(mesh.shape["region"], 4, 4, 2), ("region", "row_0", "row_1", "row_2")
    )
    in_specs = (
        P(None, REGION_ROW),
        P(None, REGION_ROW),
        P(None, REGION_ROW),
        P(REGION_ROW),
        P(REGION_ROW, None, None, None),
        P(REGION_ROW, None),
        P(REGION_ROW),
        P("region", ROW, None, None),
        P(None, REGION_ROW),
        P(None, REGION_ROW),
    )
    out_specs = (P(None, REGION_ROW), P(None, REGION_ROW), P(None, REGION_ROW))
    return jax.shard_map(local, mesh=finer, in_specs=in_specs, out_specs=out_specs, check_vma=False)
```

```python
import jax
import jax.numpy as jnp
from jax import lax
from jax.sharding import Mesh
from jax.sharding import PartitionSpec as P

STEPS = 4
ROW = ("row_0", "row_1", "row_2")
REGION_ROW = ("region", "row_0", "row_1", "row_2")


leak = 0.5


def from_each_region(chunks):
    width = chunks.shape[-1]
    padded = jnp.pad(chunks, ((0, 0), (0, 0), (0, -width % 128)))
    return lax.all_to_all(padded, "region", 0, 0, tiled=True)[..., :width]


def from_each_lane(slots):
    return lax.all_to_all(slots, ROW, 0, 0, tiled=True)


def from_every_lane(slots):
    chips = ROW[:-1]
    copies = jnp.broadcast_to(slots, (lax.axis_size(chips), *slots.shape))
    mine = lax.all_to_all(copies, chips, 0, 0, tiled=True)
    sibling = lax.ppermute(mine, ROW[-1], [(0, 1), (1, 0)])
    return jnp.stack([mine, sibling])


def split_pair(x):
    high = x.astype(jnp.bfloat16)
    low = (x - high.astype(jnp.float32)).astype(jnp.bfloat16)
    return jnp.concatenate([high, low], axis=-1)


def joined_pair(x):
    half = x.shape[-1] // 2
    return x[..., :half].astype(jnp.float32) + x[..., half:].astype(jnp.float32)


def local(
    state0,
    drive,
    cotangent,
    excitatory,
    tile_vals,
    tile_cols,
    tile_count,
    boundary_rows,
    u_factor,
    v_factor,
):
    lanes = lax.axis_size(ROW)
    groups = lax.axis_size("region")
    batch_rows, own_rows = state0.shape
    rank = v_factor.shape[0]
    own_tiles = own_rows // 128
    row_tiles = tile_vals.shape[0]
    chosen = boundary_rows.reshape(-1)
    bound_cols = chosen.shape[0]
    per_lane = own_tiles + bound_cols // 128
    tile_rows = per_lane * batch_rows
    sent = bound_cols // groups
    region_width = sent + rank
    flat_cols = tile_cols.reshape(-1)
    lane_of = flat_cols // per_lane
    cores = lax.axis_size(ROW[-1])
    side_of = (lane_of % cores != lax.axis_index(ROW[-1])).astype(jnp.int32)
    chip_of = lane_of // cores
    at_lane = flat_cols % per_lane
    live_grid = jnp.arange(tile_cols.shape[1], dtype=jnp.int32)[None, :] < tile_count[:, None]
    live_tiles = live_grid.reshape(-1)
    picks = (flat_cols[None, :] == jnp.arange(lanes * per_lane, dtype=jnp.int32)[:, None]) & live_tiles[None, :]
    picks = picks.astype(jnp.float32).reshape(lanes, per_lane, -1)
    half_rows = 16
    halves = batch_rows // half_rows
    payload_rows = tile_rows + batch_rows * 2 * rank // 128
    block_of = at_lane[:, None] * halves + jnp.arange(halves, dtype=jnp.int32)[None, :]
    picks_fwd = (
        (jnp.arange(cores, dtype=jnp.int32)[None, None, :, None, None] == side_of[:, None, None, None, None])
        & (jnp.arange(lanes // cores, dtype=jnp.int32)[None, None, None, :, None] == chip_of[:, None, None, None, None])
        & (jnp.arange(payload_rows // half_rows, dtype=jnp.int32)[None, None, None, None, :] == block_of[:, :, None, None, None])
        & live_tiles[:, None, None, None, None]
    ).astype(jnp.bfloat16)
    border_to_row = (chosen[:, None] == jnp.arange(own_rows, dtype=jnp.int32)[None, :]).astype(jnp.float32)
    row_to_border = border_to_row.T.astype(jnp.bfloat16).reshape(own_rows, groups, sent)
    polarity = (2 * excitatory - 1).astype(jnp.float32)
    drive_f = drive.astype(jnp.float32)

    def forward_start(state):
        rates = jnp.tanh(state)
        signed = (polarity * rates).astype(jnp.bfloat16)
        outgoing = jnp.einsum("bn,ndk->dbk", signed, row_to_border, preferred_element_type=jnp.float32)
        part_latent = jnp.dot(signed, v_factor.T, preferred_element_type=jnp.float32)
        chunks = jnp.concatenate(
            [
                outgoing,
                jnp.broadcast_to(part_latent, (groups, batch_rows, rank)),
            ],
            axis=2,
        )
        return rates, signed, chunks

    def forward_middle(signed, got):
        incoming = jnp.moveaxis(got[:, :, :sent], 0, 1).reshape(batch_rows, -1).astype(jnp.bfloat16)
        lane_latent = jnp.sum(got[:, :, sent:], axis=0)
        slots = jnp.concatenate(
            [
                jnp.moveaxis(signed.reshape(batch_rows, own_tiles, 128), 1, 0).reshape(-1, 128),
                incoming.reshape(batch_rows, -1),
                split_pair(lane_latent).reshape(-1, 128),
            ],
            axis=0,
        )
        return slots

    def forward_end(state, gathered):
        pair_rows = gathered[:, :, tile_rows:].reshape(lanes, batch_rows, 2 * rank)
        latent = jnp.sum(joined_pair(pair_rows), axis=0)
        stacked = gathered.reshape(*gathered.shape[:2], -1, half_rows, 128)
        blocks = jnp.einsum("shpcm,pcmrk->shrk", picks_fwd, stacked, preferred_element_type=jnp.bfloat16)
        blocks = blocks.reshape(row_tiles, -1, batch_rows, 128)
        synaptic = jnp.einsum("qjbk,qjik->bqi", blocks, tile_vals, preferred_element_type=jnp.float32)
        synaptic = synaptic.reshape(batch_rows, own_rows)
        latent_b = latent.astype(jnp.bfloat16)
        lowrank = jnp.dot(latent_b, u_factor, preferred_element_type=jnp.float32)
        return state + leak * (-state + synaptic + lowrank + drive_f), latent_b

    def adjoint_start(adjoint):
        scaled_b = (leak * adjoint).astype(jnp.bfloat16)
        part_coeff = jnp.dot(scaled_b, u_factor.T, preferred_element_type=jnp.float32)
        spread = jnp.einsum(
            "bri,rjik->brjk",
            scaled_b.reshape(batch_rows, row_tiles, 128),
            tile_vals,
            preferred_element_type=jnp.float32,
        )
        rest = spread.reshape(batch_rows, -1, 128)
        parts = []
        for _ in range(3):
            part = rest.astype(jnp.bfloat16)
            rest = rest - part.astype(jnp.float32)
            parts.append(part)
        columns = jnp.einsum(
            "lts,pbsk->ltbk", picks.astype(jnp.bfloat16), jnp.stack(parts), preferred_element_type=jnp.float32
        )
        pair_rows = split_pair(part_coeff).reshape(-1, 128)
        coeff_rows = jnp.broadcast_to(pair_rows, (lanes, *pair_rows.shape))
        tiles_rows = columns.astype(jnp.bfloat16).reshape(lanes, tile_rows, 128)
        return scaled_b, jnp.concatenate([tiles_rows, coeff_rows], axis=1)

    def adjoint_middle(got):
        everything = jnp.sum(got.astype(jnp.float32), axis=0)
        summed = everything[:tile_rows].reshape(per_lane, batch_rows, 128)
        pair_sums = everything[tile_rows:].reshape(batch_rows, 2 * rank)
        group_coeff = pair_sums[:, :rank] + pair_sums[:, rank:]
        own_part = jnp.moveaxis(summed[:own_tiles], 0, 1).reshape(batch_rows, own_rows)
        border = summed[own_tiles:].reshape(batch_rows, groups, sent)
        chunks = jnp.concatenate(
            [jnp.moveaxis(border, 1, 0), jnp.broadcast_to(group_coeff, (groups, batch_rows, rank))], axis=2
        )
        return own_part, chunks

    def adjoint_end(adjoint, own_part, back, rates):
        coeffs_b = jnp.sum(back[:, :, sent:], axis=0).astype(jnp.bfloat16)
        returned = jnp.einsum(
            "gbk,gkn->bn", back[:, :, :sent], border_to_row.reshape(groups, sent, own_rows), precision=lax.Precision.HIGHEST
        )
        through = own_part + returned
        total_signed = through + jnp.dot(coeffs_b, v_factor, preferred_element_type=jnp.float32)
        adjoint = (1.0 - leak) * adjoint + (1.0 - rates * rates) * polarity * total_signed
        return adjoint, coeffs_b

    def both_regions(first, second):
        got = from_each_region(jnp.concatenate([first, second], axis=2))
        return got[:, :, :region_width], got[:, :, region_width:]

    rates_of, signed_of, latent_of, scaled_of, coeffs_of = {}, {}, {}, {}, {}
    state = state0
    rates_of[0], signed_of[0], chunks = forward_start(state)
    got = from_each_region(chunks)
    scaled_of[3], lane_parts = adjoint_start(cotangent)
    got_last = from_each_lane(lane_parts)
    gathered = from_every_lane(forward_middle(signed_of[0], got))
    state, latent_of[0] = forward_end(state, gathered)
    own_last, chunks_last = adjoint_middle(got_last)
    rates_of[1], signed_of[1], chunks = forward_start(state)
    got, back_last = both_regions(chunks, chunks_last)
    gathered = from_every_lane(forward_middle(signed_of[1], got))
    state, latent_of[1] = forward_end(state, gathered)
    rates_of[2], signed_of[2], chunks = forward_start(state)
    got = from_each_region(chunks)
    gathered = from_every_lane(forward_middle(signed_of[2], got))
    state, latent_of[2] = forward_end(state, gathered)
    rates_of[3], signed_of[3], chunks_f3 = forward_start(state)
    adjoint, coeffs_of[3] = adjoint_end(cotangent, own_last, back_last, rates_of[3])
    scaled_of[2], lane_parts = adjoint_start(adjoint)
    own_part, chunks = adjoint_middle(from_each_lane(lane_parts))
    got_f3, back = both_regions(chunks_f3, chunks)
    adjoint, coeffs_of[2] = adjoint_end(adjoint, own_part, back, rates_of[2])
    scaled_of[1], lane_parts = adjoint_start(adjoint)
    gathered_f3 = from_every_lane(forward_middle(signed_of[3], got_f3))
    got = from_each_lane(lane_parts)
    final_state, latent_of[3] = forward_end(state, gathered_f3)
    own_part, chunks = adjoint_middle(got)
    adjoint, coeffs_of[1] = adjoint_end(adjoint, own_part, from_each_region(chunks), rates_of[1])
    scaled_of[0], lane_parts = adjoint_start(adjoint)
    own_part, chunks = adjoint_middle(from_each_lane(lane_parts))
    adjoint, coeffs_of[0] = adjoint_end(adjoint, own_part, from_each_region(chunks), rates_of[0])
    grad_u = jnp.zeros((rank, own_rows), jnp.float32)
    grad_v = jnp.zeros((rank, own_rows), jnp.float32)
    for moment in reversed(range(STEPS)):
        grad_u = grad_u + jnp.dot(latent_of[moment].T, scaled_of[moment], preferred_element_type=jnp.float32)
        grad_v = grad_v + jnp.dot(coeffs_of[moment].T, signed_of[moment], preferred_element_type=jnp.float32)
    return (final_state, grad_u, grad_v)


def solution(mesh):
    finer = Mesh(
        mesh.devices.reshape(mesh.shape["region"], 4, 4, 2), ("region", "row_0", "row_1", "row_2")
    )
    in_specs = (
        P(None, REGION_ROW),
        P(None, REGION_ROW),
        P(None, REGION_ROW),
        P(REGION_ROW),
        P(REGION_ROW, None, None, None),
        P(REGION_ROW, None),
        P(REGION_ROW),
        P("region", ROW, None, None),
        P(None, REGION_ROW),
        P(None, REGION_ROW),
    )
    out_specs = (P(None, REGION_ROW), P(None, REGION_ROW), P(None, REGION_ROW))
    return jax.shard_map(local, mesh=finer, in_specs=in_specs, out_specs=out_specs, check_vma=False)
```
